32 devices in a mesh: grp: 2 (over x), pt: 16 (over z, y, core).
Axes of the slice: x: 2, y: 2, z: 4, core: 2. Of those that a mesh axis runs over, the one named last changes fastest.
Arguments:
- left_factor: float32 [16, 128, 2048], P('grp', 'pt'), may hold values from 0 to 7340032, as said below
- right_factor: float32 [128, 128, 2048], P('grp', 'pt'), may hold values from 0 to 7340032, as said below
Outputs:
- product: float32 [16, 128, 4096], P('grp', 'pt')
The draws below stay inside these ranges and needn't reach their ends.
Inputs may be any that keep to these rules, and one draw needn't show every extreme that they name: `left_factor`: every entry is a whole number, a residue modulo 7340033. `right_factor`: every entry is a whole number, a residue modulo 7340033.
All inputs are finite; a program needn't handle non-finite values.
Results may differ from the reference program's by a relative error of at most 0.0003.
Values sent between devices are 32-bit elements; how exact they have to be, the bound alone decides.
No kernel may reach another device: no remote copies, remote signals or barrier semaphores. Data moves between devices by JAX's collectives and lax.ppermute only.
A program may use at most 192 MiB of HBM per device.

```python
import jax
import jax.numpy as jnp
import numpy as np
from jax import lax

ORDER = 128
LEFT_ROWS = 16
FIRST = 32
SECOND = 128
COEFFS = 2048


modulus = 7340033


def residues(key, array_shape):
    values = jax.random.randint(key, array_shape, 0, modulus)
    corner = (lax.broadcasted_iota(jnp.int32, array_shape, 0) == 0) & (lax.broadcasted_iota(jnp.int32, array_shape, 1) == 0)
    last_pos = lax.broadcasted_iota(jnp.int32, array_shape, 2)
    values = jnp.where(corner & (last_pos == 0), modulus - 1, values)
    values = jnp.where(corner & (last_pos == 1), 0, values)
    return values.astype(jnp.float32)


def draw_left_factor(key, part):
    return residues(jax.random.fold_in(key, 11), (LEFT_ROWS, ORDER, COEFFS))


def draw_right_factor(key, part):
    return residues(jax.random.fold_in(key, 23), (ORDER, ORDER, COEFFS))


def setup_inputs(seed: int = 0) -> dict:
    seeds = jax.random.split(jax.random.key(seed), 3)
    left_factor = draw_left_factor(jax.random.fold_in(seeds[2], 71), 0)
    right_factor = draw_right_factor(jax.random.fold_in(seeds[2], 71), 0)
    return dict(left_factor=left_factor, right_factor=right_factor)


modulus = 7340033


def root_powers(length_all):
    for generator in range(2, 64):
        candidate = pow(generator, (modulus - 1) // length_all, modulus)
        if pow(candidate, length_all // 2, modulus) == modulus - 1:
            break
    powers = [1]
    for counter in range(length_all - 1):
        powers.append(powers[-1] * candidate % modulus)
    return np.array(powers, dtype=np.int64)


def power_table(powers, exponents):
    return powers[exponents % powers.shape[0]]


def dft_tables():
    length_all = FIRST * SECOND
    powers = root_powers(length_all)
    half_first = np.arange(FIRST // 2)
    range_first = np.arange(FIRST)
    range_second = np.arange(SECOND)
    first_table = power_table(powers, SECOND * np.outer(half_first, range_first))
    twist_table = power_table(powers, np.outer(range_first, range_second))
    second_table = power_table(powers, FIRST * np.outer(range_second, range_second))
    back_first_table = power_table(powers, -FIRST * np.outer(range_second, range_second))
    back_twist_table = power_table(powers, -np.outer(range_second, range_first))
    scale_inv = pow(length_all, modulus - 2, modulus)
    back_second_table = power_table(powers, -SECOND * np.outer(range_first, range_first)) * scale_inv % modulus
    return (first_table, twist_table, second_table, back_first_table, back_twist_table, back_second_table)


def stacked_table(table_np):
    pieces = [(table_np // (256 ** limb_level)) % 256 for limb_level in range(3)]
    stacked = np.zeros((5, 3) + table_np.shape, dtype=np.float32)
    for total_level in range(5):
        for limb_level in range(3):
            partner = total_level - limb_level
            if 0 <= partner < 3:
                stacked[total_level, limb_level] = pieces[partner]
    return stacked


def limb_split(values):
    return [values % 256, (values // 256) % 256, values // 65536]


def fold_sums(level_sums):
    result = level_sums[4] % modulus
    for limb_level in (3, 2, 1, 0):
        result = (result * 256 + level_sums[limb_level]) % modulus
    return result


def times_table(values, table_np):
    left_limbs = limb_split(values)
    right_limbs = limb_split(jnp.asarray(table_np.astype(np.int32)))
    level_sums = []
    for total_level in range(5):
        running = jnp.zeros_like(values)
        for limb_level in range(3):
            partner = total_level - limb_level
            if 0 <= partner < 3:
                running = running + left_limbs[limb_level] * right_limbs[partner]
        level_sums.append(running)
    return fold_sums(level_sums)


def limb_stack(values):
    return jnp.stack([piece.astype(jnp.float32) for piece in limb_split(values)])


def contract(form, values, table_np):
    planes = jnp.einsum(form, limb_stack(values), jnp.asarray(stacked_table(table_np), jnp.float32), precision=lax.Precision.HIGHEST)
    return fold_sums([planes[limb_level].astype(jnp.int32) for limb_level in range(5)])


def forward(rows_in, tables):
    first_table, twist_table, second_table = tables[0], tables[1], tables[2]
    entries = rows_in.shape[0]
    current = rows_in.reshape(entries, FIRST // 2, SECOND)
    current = contract("leab,slac->secb", current, first_table)
    current = times_table(current, twist_table)
    current = contract("lecb,slbd->sdce", current, second_table)
    return current.reshape(FIRST * SECOND, entries)


def inverse(point_values, tables):
    back_first_table, back_twist_table, back_second_table = tables[3], tables[4], tables[5]
    entries = point_values.shape[1]
    current = point_values.reshape(SECOND, FIRST, entries)
    current = contract("ldce,sldb->sebc", current, back_first_table)
    current = times_table(current, back_twist_table)
    current = contract("lebc,slca->seab", current, back_second_table)
    return current.reshape(entries, FIRST * SECOND)


def multiply_points(left_points, right_points):
    planes = jnp.einsum("xpik,ypjk->xypij", limb_stack(left_points), limb_stack(right_points), precision=lax.Precision.HIGHEST)
    level_sums = []
    for total_level in range(5):
        running = jnp.zeros(planes.shape[2:], jnp.int32)
        for limb_level in range(3):
            partner = total_level - limb_level
            if 0 <= partner < 3:
                running = running + planes[limb_level, partner].astype(jnp.int32)
        level_sums.append(running)
    return fold_sums(level_sums)


def reference(left_factor, right_factor):
    tables = dft_tables()

    def evaluate(entry_block):
        return forward(entry_block, tables)

    def to_points(factor):
        blocks = factor.astype(jnp.int32).reshape(-1, ORDER, COEFFS)
        return jnp.moveaxis(lax.map(evaluate, blocks), 0, 1)

    left_points = to_points(left_factor)
    right_points = to_points(right_factor)

    def multiply(pair_in):
        return multiply_points(pair_in[0], pair_in[1])

    products = lax.map(multiply, (left_points.reshape(SECOND, FIRST, LEFT_ROWS, ORDER), right_points.reshape(SECOND, FIRST, ORDER, ORDER)))
    moved = jnp.moveaxis(products.reshape(FIRST * SECOND, LEFT_ROWS, ORDER), 1, 0)

    def interpolate(entry_block):
        return inverse(entry_block, tables)

    coefficients = lax.map(interpolate, moved)
    return coefficients.astype(jnp.float32) / modulus
```

```python
import jax
import jax.numpy as jnp
import numpy as np
from jax import lax
from jax.sharding import PartitionSpec as P

FIRST = 32
SECOND = 128
HALF_FIRST = FIRST // 2
LENGTH = FIRST * SECOND

modulus = 7340033
INV_P = float(np.float32(1.0 / modulus))


def root_powers(length_all):
    for generator in range(2, 64):
        candidate = pow(generator, (modulus - 1) // length_all, modulus)
        if pow(candidate, length_all // 2, modulus) == modulus - 1:
            break
    powers = [1]
    for counter in range(length_all - 1):
        powers.append(powers[-1] * candidate % modulus)
    return np.array(powers, dtype=np.int64)


def balanced_limbs(values):
    v = np.asarray(values, dtype=np.int64)
    l0 = (v + 128) % 256 - 128
    v = (v - l0) // 256
    l1 = (v + 128) % 256 - 128
    l2 = (v - l1) // 256
    return [l0, l1, l2]


def scaled_stack(table):
    n, k = table.shape
    out = np.zeros((3, n, 3, k), dtype=np.float32)
    for level in range(3):
        scaled = table * pow(256, level, modulus) % modulus
        for limb, piece in enumerate(balanced_limbs(scaled)):
            out[limb, :, level, :] = piece
    return out.reshape(3 * n, 3 * k)


def twist_stack(table):
    out = np.zeros((3, 3) + table.shape, dtype=np.float32)
    for level in range(3):
        scaled = table * pow(256, level, modulus) % modulus
        for limb, piece in enumerate(balanced_limbs(scaled)):
            out[level, limb] = piece
    return out


def build_tables():
    powers = root_powers(LENGTH)

    def pw(e):
        return powers[np.asarray(e) % LENGTH]

    a16 = np.arange(HALF_FIRST)
    c32 = np.arange(FIRST)
    b128 = np.arange(SECOND)
    scale_inv = pow(LENGTH, modulus - 2, modulus)
    fwd1 = pw(SECOND * np.outer(c32, a16))
    fwd_twist = pw(np.outer(c32, b128))
    fwd2 = pw(FIRST * np.outer(b128, b128))
    inv1 = pw(-FIRST * np.outer(b128, b128))
    inv_twist = pw(-np.outer(c32, b128))
    inv2 = pw(-SECOND * np.outer(c32, c32)) * scale_inv % modulus
    return dict(
        fwd1=scaled_stack(fwd1),
        fwd_twist=twist_stack(fwd_twist),
        fwd2=scaled_stack(fwd2).T.copy(),
        inv1=scaled_stack(inv1).T.copy(),
        inv_twist=twist_stack(inv_twist),
        inv2=scaled_stack(inv2),
    )


def split3(x):
    h = jnp.floor(x * (1.0 / 256.0))
    x0 = x - 256.0 * h
    x2 = jnp.floor(h * (1.0 / 256.0))
    x1 = h - 256.0 * x2
    return x0, x1, x2


def fold3(s0, s1, s2):
    f = s2 * 65536.0 + s1 * 256.0 + s0
    q = jnp.round(f * INV_P)
    d = s2 - 112.0 * q
    e = s1 + 256.0 * d
    r = s0 + 256.0 * e - q
    return jnp.where(r < 0, r + float(modulus), r)


def twist(z, tw):
    zl = split3(z)
    s = [zl[0] * tw[0, u] + zl[1] * tw[1, u] + zl[2] * tw[2, u] for u in range(3)]
    return fold3(*s)


def limbs_bf16(x, axis):
    return jnp.concatenate([piece.astype(jnp.bfloat16) for piece in split3(x)], axis=axis)


def forward(x, tables):
    entries = x.shape[0]
    x = x.reshape(entries, HALF_FIRST, SECOND)
    xl = limbs_bf16(x, 1)
    y = jnp.einsum(
        "eLb,NL->eNb", xl, jnp.asarray(tables["fwd1"], jnp.bfloat16), preferred_element_type=jnp.float32
    )
    z = fold3(y[:, 0:FIRST], y[:, FIRST : 2 * FIRST], y[:, 2 * FIRST :])
    z = twist(z, jnp.asarray(tables["fwd_twist"]))
    zl = limbs_bf16(z, 2)
    y2 = jnp.einsum(
        "ecK,KN->ecN", zl, jnp.asarray(tables["fwd2"], jnp.bfloat16), preferred_element_type=jnp.float32
    )
    return fold3(y2[..., 0:SECOND], y2[..., SECOND : 2 * SECOND], y2[..., 2 * SECOND :])


def inverse(pv, tables):
    entries = pv.shape[0]
    pl_ = limbs_bf16(pv, 2)
    y = jnp.einsum(
        "ecK,KN->ecN", pl_, jnp.asarray(tables["inv1"], jnp.bfloat16), preferred_element_type=jnp.float32
    )
    z = fold3(y[..., 0:SECOND], y[..., SECOND : 2 * SECOND], y[..., 2 * SECOND :])
    z = twist(z, jnp.asarray(tables["inv_twist"]))
    zl = limbs_bf16(z, 1)
    y2 = jnp.einsum(
        "eLb,NL->eNb", zl, jnp.asarray(tables["inv2"], jnp.bfloat16), preferred_element_type=jnp.float32
    )
    out = fold3(y2[:, 0:FIRST], y2[:, FIRST : 2 * FIRST], y2[:, 2 * FIRST :])
    return out.reshape(entries, LENGTH)


def multiply_points(left, right):
    ll = jnp.stack([v.astype(jnp.bfloat16) for v in split3(left)])
    rl = jnp.stack([v.astype(jnp.bfloat16) for v in split3(right)])
    planes = jnp.einsum("xpik,ypjk->xypij", ll, rl, preferred_element_type=jnp.float32)
    lv0 = planes[0, 0]
    lv1 = planes[0, 1] + planes[1, 0]
    lv2 = planes[0, 2] + planes[1, 1] + planes[2, 0]
    lv3 = planes[1, 2] + planes[2, 1]
    lv4 = planes[2, 2]
    high = fold3(lv2, lv3, lv4)
    return fold3(lv0, lv1, high)


def make_body(n_grp, n_pt):
    tables = build_tables()
    d_local = SECOND // n_pt
    half = n_pt // n_grp

    def body(left_factor, right_factor):
        il, kl, _ = left_factor.shape
        jl = right_factor.shape[0]
        left_eval = forward(left_factor.reshape(il * kl, -1), tables)
        right_eval = forward(right_factor.reshape(jl * kl, -1), tables)

        def to_points(ev, rows):
            ev = ev.reshape(rows, kl, FIRST, n_pt, d_local)
            ev = jnp.transpose(ev, (3, 2, 4, 0, 1))
            ev = lax.all_to_all(ev, "pt", split_axis=0, concat_axis=4, tiled=True)
            return ev.reshape(FIRST * d_local, rows, n_pt * kl)

        left_pts = to_points(left_eval, il)
        left_pts = lax.all_gather(left_pts, "grp", axis=1, tiled=True)
        right_pts = to_points(right_eval, jl)
        prod = multiply_points(left_pts, right_pts)
        n_i = prod.shape[1]
        ib = n_i // n_grp
        jb = jl // half
        prod = prod.reshape(FIRST, d_local, n_grp, ib, half, jb)
        prod = jnp.transpose(prod, (2, 4, 0, 1, 3, 5))
        prod = prod.reshape(n_pt, FIRST, d_local, ib, jb)
        prod = lax.all_to_all(prod, "pt", split_axis=0, concat_axis=0, tiled=False)
        perm = []
        for h in range(n_grp):
            for q in range(n_pt):
                g_o, r = q // half, q % half
                perm.append((h * n_pt + q, g_o * n_pt + h * half + r))
        prod = lax.ppermute(prod, ("grp", "pt"), perm)
        pv = jnp.transpose(prod, (3, 4, 1, 0, 2)).reshape(ib * jb, FIRST, SECOND)
        coeffs = inverse(pv, tables)
        return (coeffs / float(modulus)).reshape(ib, jb, LENGTH)

    return body


def solution(mesh):
    n_grp = mesh.shape["grp"]
    n_pt = mesh.shape["pt"]
    return jax.shard_map(
        make_body(n_grp, n_pt),
        mesh=mesh,
        in_specs=(P("grp", "pt", None), P("grp", "pt", None)),
        out_specs=P("grp", "pt", None),
        check_vma=False,
    )
```

```python
import jax
import jax.numpy as jnp
import numpy as np
from jax import lax
from jax.sharding import PartitionSpec as P

FIRST = 32
SECOND = 128
HALF_FIRST = FIRST // 2
LENGTH = FIRST * SECOND

modulus = 7340033
INV_P = float(np.float32(1.0 / modulus))


def root_powers(length_all):
    for generator in range(2, 64):
        candidate = pow(generator, (modulus - 1) // length_all, modulus)
        if pow(candidate, length_all // 2, modulus) == modulus - 1:
            break
    powers = [1]
    for counter in range(length_all - 1):
        powers.append(powers[-1] * candidate % modulus)
    return np.array(powers, dtype=np.int64)


def balanced_limbs(values):
    v = np.asarray(values, dtype=np.int64)
    l0 = (v + 128) % 256 - 128
    v = (v - l0) // 256
    l1 = (v + 128) % 256 - 128
    l2 = (v - l1) // 256
    return [l0, l1, l2]


def scaled_stack(table):
    n, k = table.shape
    out = np.zeros((3, n, 3, k), dtype=np.float32)
    for level in range(3):
        scaled = table * pow(256, level, modulus) % modulus
        for limb, piece in enumerate(balanced_limbs(scaled)):
            out[limb, :, level, :] = piece
    return out.reshape(3 * n, 3 * k)


def twist_stack(table):
    out = np.zeros((3, 3) + table.shape, dtype=np.float32)
    for level in range(3):
        scaled = table * pow(256, level, modulus) % modulus
        for limb, piece in enumerate(balanced_limbs(scaled)):
            out[level, limb] = piece
    return out


def build_tables():
    powers = root_powers(LENGTH)

    def pw(e):
        return powers[np.asarray(e) % LENGTH]

    a16 = np.arange(HALF_FIRST)
    c32 = np.arange(FIRST)
    b128 = np.arange(SECOND)
    scale_inv = pow(LENGTH, modulus - 2, modulus)
    fwd1 = pw(SECOND * np.outer(c32, a16))
    fwd_twist = pw(np.outer(c32, b128))
    fwd2 = pw(FIRST * np.outer(b128, b128))
    inv1 = pw(-FIRST * np.outer(b128, b128))
    inv_twist = pw(-np.outer(c32, b128))
    inv2 = pw(-SECOND * np.outer(c32, c32)) * scale_inv % modulus
    return dict(
        fwd1=scaled_stack(fwd1),
        fwd_twist=twist_stack(fwd_twist),
        fwd2=scaled_stack(fwd2).T.copy(),
        inv1=scaled_stack(inv1).T.copy(),
        inv_twist=twist_stack(inv_twist),
        inv2=scaled_stack(inv2),
    )


def split3(x):
    h = jnp.floor(x * (1.0 / 256.0))
    x0 = x - 256.0 * h
    x2 = jnp.floor(h * (1.0 / 256.0))
    x1 = h - 256.0 * x2
    return x0, x1, x2


def fold3(s0, s1, s2):
    f = s2 * 65536.0 + s1 * 256.0 + s0
    q = jnp.round(f * INV_P)
    d = s2 - 112.0 * q
    e = s1 + 256.0 * d
    r = s0 + 256.0 * e - q
    return jnp.where(r < 0, r + float(modulus), r)


def twist(z, tw):
    zl = split3(z)
    s = [zl[0] * tw[0, u] + zl[1] * tw[1, u] + zl[2] * tw[2, u] for u in range(3)]
    return fold3(*s)


def limbs_bf16(x, axis):
    return jnp.concatenate([piece.astype(jnp.bfloat16) for piece in split3(x)], axis=axis)


def forward(x, tables):
    entries = x.shape[0]
    x = x.reshape(entries, HALF_FIRST, SECOND)
    xl = limbs_bf16(x, 1)
    y = jnp.einsum(
        "eLb,NL->eNb", xl, jnp.asarray(tables["fwd1"], jnp.bfloat16), preferred_element_type=jnp.float32
    )
    z = fold3(y[:, 0:FIRST], y[:, FIRST : 2 * FIRST], y[:, 2 * FIRST :])
    z = twist(z, jnp.asarray(tables["fwd_twist"]))
    zl = limbs_bf16(z, 2)
    y2 = jnp.einsum(
        "ecK,KN->ecN", zl, jnp.asarray(tables["fwd2"], jnp.bfloat16), preferred_element_type=jnp.float32
    )
    return fold3(y2[..., 0:SECOND], y2[..., SECOND : 2 * SECOND], y2[..., 2 * SECOND :])


def inverse(pv, tables):
    entries = pv.shape[0]
    pl_ = limbs_bf16(pv, 2)
    y = jnp.einsum(
        "ecK,KN->ecN", pl_, jnp.asarray(tables["inv1"], jnp.bfloat16), preferred_element_type=jnp.float32
    )
    z = fold3(y[..., 0:SECOND], y[..., SECOND : 2 * SECOND], y[..., 2 * SECOND :])
    z = twist(z, jnp.asarray(tables["inv_twist"]))
    zl = limbs_bf16(z, 1)
    y2 = jnp.einsum(
        "eLb,NL->eNb", zl, jnp.asarray(tables["inv2"], jnp.bfloat16), preferred_element_type=jnp.float32
    )
    out = fold3(y2[:, 0:FIRST], y2[:, FIRST : 2 * FIRST], y2[:, 2 * FIRST :])
    return out.reshape(entries, LENGTH)


def multiply_points(left, right):
    left_limbs = [v.astype(jnp.bfloat16) for v in split3(left)]
    zero = jnp.zeros_like(left_limbs[0])
    rows = []
    for level in range(5):
        pieces = [left_limbs[level - y] if 0 <= level - y < 3 else zero for y in range(3)]
        rows.append(jnp.concatenate(pieces, axis=2))
    toeplitz = jnp.concatenate(rows, axis=1)
    right_limbs = limbs_bf16(right, 2)
    levels = jnp.einsum("pak,pjk->paj", toeplitz, right_limbs, preferred_element_type=jnp.float32)
    n_i = left.shape[1]
    lv = [levels[:, n * n_i : (n + 1) * n_i] for n in range(5)]
    high = fold3(lv[2], lv[3], lv[4])
    return fold3(lv[0], lv[1], high)


def make_body(n_grp, n_pt):
    tables = build_tables()
    d_local = SECOND // n_pt

    def body(left_factor, right_factor):
        il, kl, _ = left_factor.shape
        jl = right_factor.shape[0]
        left_eval = forward(left_factor.reshape(il * kl, -1), tables)
        right_eval = forward(right_factor.reshape(jl * kl, -1), tables)

        def to_points(ev, rows):
            ev = ev.reshape(rows, kl, FIRST, n_pt, d_local)
            ev = jnp.transpose(ev, (3, 2, 4, 0, 1))
            ev = lax.all_to_all(ev, "pt", split_axis=0, concat_axis=4, tiled=True)
            return ev.reshape(FIRST * d_local, rows, n_pt * kl)

        left_pts = to_points(left_eval, il)
        left_pts = jnp.broadcast_to(left_pts[None], (n_grp,) + left_pts.shape)
        left_pts = lax.all_to_all(left_pts, "grp", split_axis=0, concat_axis=0, tiled=True)
        left_pts = jnp.transpose(left_pts, (1, 0, 2, 3)).reshape(FIRST * d_local, n_grp * il, n_pt * kl)
        right_pts = to_points(right_eval, jl)
        prod = multiply_points(left_pts, right_pts)
        n_i = prod.shape[1]
        ib = n_i // n_grp
        jb = n_grp * jl // n_pt
        prod = prod.reshape(FIRST * d_local, n_grp, ib, jl)
        prod = lax.all_to_all(prod, "grp", split_axis=1, concat_axis=1, tiled=True)
        prod = jnp.transpose(prod, (0, 2, 1, 3)).reshape(FIRST, d_local, ib, n_pt, jb)
        prod = jnp.transpose(prod, (3, 0, 1, 2, 4))
        prod = lax.all_to_all(prod, "pt", split_axis=0, concat_axis=0, tiled=False)
        pv = jnp.transpose(prod, (3, 4, 1, 0, 2)).reshape(ib * jb, FIRST, SECOND)
        coeffs = inverse(pv, tables)
        return (coeffs / float(modulus)).reshape(ib, jb, LENGTH)

    return body


def solution(mesh):
    n_grp = mesh.shape["grp"]
    n_pt = mesh.shape["pt"]
    return jax.shard_map(
        make_body(n_grp, n_pt),
        mesh=mesh,
        in_specs=(P("grp", "pt", None), P("grp", "pt", None)),
        out_specs=P("grp", "pt", None),
        check_vma=False,
    )
```

```python
import jax
import jax.numpy as jnp
import numpy as np
from jax import lax
from jax.sharding import PartitionSpec as P

FIRST = 32
SECOND = 128
HALF_FIRST = FIRST // 2
LENGTH = FIRST * SECOND

modulus = 7340033
INV_P = float(np.float32(1.0 / modulus))


def root_powers(length_all):
    for generator in range(2, 64):
        candidate = pow(generator, (modulus - 1) // length_all, modulus)
        if pow(candidate, length_all // 2, modulus) == modulus - 1:
            break
    powers = [1]
    for counter in range(length_all - 1):
        powers.append(powers[-1] * candidate % modulus)
    return np.array(powers, dtype=np.int64)


def balanced_limbs(values):
    v = np.asarray(values, dtype=np.int64)
    l0 = (v + 128) % 256 - 128
    v = (v - l0) // 256
    l1 = (v + 128) % 256 - 128
    l2 = (v - l1) // 256
    return [l0, l1, l2]


def scaled_stack(table):
    n, k = table.shape
    out = np.zeros((3, n, 3, k), dtype=np.float32)
    for level in range(3):
        scaled = table * pow(256, level, modulus) % modulus
        for limb, piece in enumerate(balanced_limbs(scaled)):
            out[limb, :, level, :] = piece
    return out.reshape(3 * n, 3 * k)


def twist_stack(table):
    out = np.zeros((3, 3) + table.shape, dtype=np.float32)
    for level in range(3):
        scaled = table * pow(256, level, modulus) % modulus
        for limb, piece in enumerate(balanced_limbs(scaled)):
            out[level, limb] = piece
    return out


def build_tables():
    powers = root_powers(LENGTH)

    def pw(e):
        return powers[np.asarray(e) % LENGTH]

    a16 = np.arange(HALF_FIRST)
    c32 = np.arange(FIRST)
    b128 = np.arange(SECOND)
    scale_inv = pow(LENGTH, modulus - 2, modulus)
    fwd1 = pw(SECOND * np.outer(c32, a16))
    fwd_twist = pw(np.outer(c32, b128))
    fwd2 = pw(FIRST * np.outer(b128, b128))
    inv1 = pw(-FIRST * np.outer(b128, b128))
    inv_twist = pw(-np.outer(c32, b128))
    inv2 = pw(-SECOND * np.outer(c32, c32)) * scale_inv % modulus
    return dict(
        fwd1=scaled_stack(fwd1),
        fwd_twist=twist_stack(fwd_twist),
        fwd2=scaled_stack(fwd2).T.copy(),
        inv1=scaled_stack(inv1).T.copy(),
        inv_twist=twist_stack(inv_twist),
        inv2=scaled_stack(inv2),
    )


def split3(x):
    h = jnp.floor(x * (1.0 / 256.0))
    x0 = x - 256.0 * h
    x2 = jnp.floor(h * (1.0 / 256.0))
    x1 = h - 256.0 * x2
    return x0, x1, x2


def fold3(s0, s1, s2):
    f = s2 * 65536.0 + s1 * 256.0 + s0
    q = jnp.round(f * INV_P)
    d = s2 - 112.0 * q
    e = s1 + 256.0 * d
    r = s0 + 256.0 * e - q
    return jnp.where(r < 0, r + float(modulus), r)


def twist(z, tw):
    zl = split3(z)
    s = [zl[0] * tw[0, u] + zl[1] * tw[1, u] + zl[2] * tw[2, u] for u in range(3)]
    return fold3(*s)


def limbs_bf16(x, axis):
    return jnp.concatenate([piece.astype(jnp.bfloat16) for piece in split3(x)], axis=axis)


def forward(x, tables):
    entries = x.shape[0]
    x = x.reshape(entries, HALF_FIRST, SECOND)
    xl = limbs_bf16(x, 1)
    y = jnp.einsum(
        "eLb,NL->eNb", xl, jnp.asarray(tables["fwd1"], jnp.bfloat16), preferred_element_type=jnp.float32
    )
    z = fold3(y[:, 0:FIRST], y[:, FIRST : 2 * FIRST], y[:, 2 * FIRST :])
    z = twist(z, jnp.asarray(tables["fwd_twist"]))
    zl = limbs_bf16(z, 2)
    y2 = jnp.einsum(
        "ecK,KN->Nec", zl, jnp.asarray(tables["fwd2"], jnp.bfloat16), preferred_element_type=jnp.float32
    )
    return fold3(y2[0:SECOND], y2[SECOND : 2 * SECOND], y2[2 * SECOND :])


def inverse(pv, tables):
    entries = pv.shape[0]
    pl_ = limbs_bf16(pv, 2)
    y = jnp.einsum(
        "ecK,KN->ecN", pl_, jnp.asarray(tables["inv1"], jnp.bfloat16), preferred_element_type=jnp.float32
    )
    z = fold3(y[..., 0:SECOND], y[..., SECOND : 2 * SECOND], y[..., 2 * SECOND :])
    z = twist(z, jnp.asarray(tables["inv_twist"]))
    zl = limbs_bf16(z, 1)
    y2 = jnp.einsum(
        "eLb,NL->eNb", zl, jnp.asarray(tables["inv2"], jnp.bfloat16), preferred_element_type=jnp.float32
    )
    out = fold3(y2[:, 0:FIRST], y2[:, FIRST : 2 * FIRST], y2[:, 2 * FIRST :])
    return out.reshape(entries, LENGTH)


def multiply_points(left, right):
    left_limbs = [v.astype(jnp.bfloat16) for v in split3(left)]
    zero = jnp.zeros_like(left_limbs[0])
    rows = []
    for level in range(5):
        pieces = [left_limbs[level - y] if 0 <= level - y < 3 else zero for y in range(3)]
        rows.append(jnp.concatenate(pieces, axis=2))
    toeplitz = jnp.concatenate(rows, axis=1)
    right_limbs = limbs_bf16(right, 2)
    levels = jnp.einsum("pak,pjk->paj", toeplitz, right_limbs, preferred_element_type=jnp.float32)
    n_i = left.shape[1]
    lv = [levels[:, n * n_i : (n + 1) * n_i] for n in range(5)]
    high = fold3(lv[2], lv[3], lv[4])
    return fold3(lv[0], lv[1], high)


def make_body(n_grp, n_pt, n_chunks):
    tables = build_tables()
    d_local = SECOND // n_pt

    def body(left_factor, right_factor):
        il, kl, _ = left_factor.shape
        jl = right_factor.shape[0]

        def to_points(x, rows):
            ev = forward(x.reshape(rows * kl, -1), tables)
            ev = ev.reshape(n_pt, d_local, rows, kl, FIRST)
            ev = lax.all_to_all(ev, "pt", split_axis=0, concat_axis=0, tiled=False)
            return ev

        left_pts = to_points(left_factor, il)
        left_pts = jnp.broadcast_to(left_pts[None], (n_grp,) + left_pts.shape)
        left_pts = lax.all_to_all(left_pts, "grp", split_axis=0, concat_axis=0, tiled=True)
        left_pts = jnp.transpose(left_pts, (2, 5, 0, 3, 1, 4))
        left_pts = left_pts.reshape(d_local * FIRST, n_grp * il, n_pt * kl)
        jc = jl // n_chunks
        prods = []
        for chunk in range(n_chunks):
            right_pts = to_points(right_factor[chunk * jc : (chunk + 1) * jc], jc)
            right_pts = jnp.transpose(right_pts, (1, 4, 2, 0, 3)).reshape(d_local * FIRST, jc, n_pt * kl)
            prods.append(multiply_points(left_pts, right_pts))
        prod = jnp.concatenate(prods, axis=2) if n_chunks > 1 else prods[0]
        n_i = prod.shape[1]
        ib = n_i // n_grp
        jb = n_grp * jl // n_pt
        prod = prod.reshape(d_local * FIRST, n_grp, ib, jl)
        prod = lax.all_to_all(prod, "grp", split_axis=1, concat_axis=1, tiled=True)
        prod = jnp.transpose(prod, (0, 2, 1, 3)).reshape(d_local, FIRST, ib, n_pt, jb)
        prod = jnp.transpose(prod, (3, 0, 1, 2, 4))
        prod = lax.all_to_all(prod, "pt", split_axis=0, concat_axis=0, tiled=False)
        pv = jnp.transpose(prod, (3, 4, 2, 0, 1)).reshape(ib * jb, FIRST, SECOND)
        coeffs = inverse(pv, tables)
        return (coeffs / float(modulus)).reshape(ib, jb, LENGTH)

    return body


def solution(mesh):
    n_grp = mesh.shape["grp"]
    n_pt = mesh.shape["pt"]
    return jax.shard_map(
        make_body(n_grp, n_pt, 4),
        mesh=mesh,
        in_specs=(P("grp", "pt", None), P("grp", "pt", None)),
        out_specs=P("grp", "pt", None),
        check_vma=False,
    )
```

```python
import jax
import jax.numpy as jnp
import numpy as np
from jax import lax
from jax.sharding import PartitionSpec as P

FIRST = 32
SECOND = 128
HALF_FIRST = FIRST // 2
LENGTH = FIRST * SECOND

modulus = 7340033
INV_P = float(np.float32(1.0 / modulus))


def root_powers(length_all):
    for generator in range(2, 64):
        candidate = pow(generator, (modulus - 1) // length_all, modulus)
        if pow(candidate, length_all // 2, modulus) == modulus - 1:
            break
    powers = [1]
    for counter in range(length_all - 1):
        powers.append(powers[-1] * candidate % modulus)
    return np.array(powers, dtype=np.int64)


def balanced_limbs(values):
    v = np.asarray(values, dtype=np.int64)
    l0 = (v + 128) % 256 - 128
    v = (v - l0) // 256
    l1 = (v + 128) % 256 - 128
    l2 = (v - l1) // 256
    return [l0, l1, l2]


def scaled_stack(table):
    n, k = table.shape
    out = np.zeros((3, n, 3, k), dtype=np.float32)
    for level in range(3):
        scaled = table * pow(256, level, modulus) % modulus
        for limb, piece in enumerate(balanced_limbs(scaled)):
            out[limb, :, level, :] = piece
    return out.reshape(3 * n, 3 * k)


def twist_stack(table):
    out = np.zeros((3, 3) + table.shape, dtype=np.float32)
    for level in range(3):
        scaled = table * pow(256, level, modulus) % modulus
        for limb, piece in enumerate(balanced_limbs(scaled)):
            out[level, limb] = piece
    return out


def build_tables():
    powers = root_powers(LENGTH)

    def pw(e):
        return powers[np.asarray(e) % LENGTH]

    a16 = np.arange(HALF_FIRST)
    c32 = np.arange(FIRST)
    b128 = np.arange(SECOND)
    scale_inv = pow(LENGTH, modulus - 2, modulus)
    fwd1 = pw(SECOND * np.outer(c32, a16))
    fwd_twist = pw(np.outer(c32, b128))
    fwd2 = pw(FIRST * np.outer(b128, b128))
    inv1 = pw(-FIRST * np.outer(b128, b128))
    inv_twist = pw(-np.outer(b128, c32))
    inv2 = pw(-SECOND * np.outer(c32, c32)) * scale_inv % modulus
    return dict(
        fwd1=scaled_stack(fwd1),
        fwd_twist=twist_stack(fwd_twist)[..., None],
        fwd2=scaled_stack(fwd2),
        inv1=scaled_stack(inv1),
        inv_twist=twist_stack(inv_twist)[..., None],
        inv2=scaled_stack(inv2),
    )


def split3(x):
    h = jnp.floor(x * (1.0 / 256.0))
    x0 = x - 256.0 * h
    x2 = jnp.floor(h * (1.0 / 256.0))
    x1 = h - 256.0 * x2
    return x0, x1, x2


def fold3(s0, s1, s2):
    f = s2 * 65536.0 + s1 * 256.0 + s0
    q = jnp.round(f * INV_P)
    d = s2 - 112.0 * q
    e = s1 + 256.0 * d
    r = s0 + 256.0 * e - q
    return jnp.where(r < 0, r + float(modulus), r)


def twist(z, tw):
    zl = split3(z)
    s = [zl[0] * tw[0, u] + zl[1] * tw[1, u] + zl[2] * tw[2, u] for u in range(3)]
    return fold3(*s)


def limbs_bf16(x, axis):
    return jnp.concatenate([piece.astype(jnp.bfloat16) for piece in split3(x)], axis=axis)


def bf16_table(tables, name):
    return jnp.asarray(tables[name], jnp.bfloat16)


def forward(xt, tables):
    entries = xt.shape[1]
    x = xt.reshape(HALF_FIRST, SECOND, entries)
    xl = limbs_bf16(x, 0)
    y = jnp.einsum("NK,Kbe->Nbe", bf16_table(tables, "fwd1"), xl, preferred_element_type=jnp.float32)
    z = fold3(y[0:FIRST], y[FIRST : 2 * FIRST], y[2 * FIRST :])
    z = twist(z, jnp.asarray(tables["fwd_twist"]))
    zl = limbs_bf16(z, 1)
    y2 = jnp.einsum("NK,cKe->cNe", bf16_table(tables, "fwd2"), zl, preferred_element_type=jnp.float32)
    return fold3(y2[:, 0:SECOND], y2[:, SECOND : 2 * SECOND], y2[:, 2 * SECOND :])


def inverse(pv, tables):
    pl_ = limbs_bf16(pv, 0)
    y = jnp.einsum("NK,Kce->Nce", bf16_table(tables, "inv1"), pl_, preferred_element_type=jnp.float32)
    z = fold3(y[0:SECOND], y[SECOND : 2 * SECOND], y[2 * SECOND :])
    z = twist(z, jnp.asarray(tables["inv_twist"]))
    zl = limbs_bf16(z, 1)
    y2 = jnp.einsum("NK,bKe->bNe", bf16_table(tables, "inv2"), zl, preferred_element_type=jnp.float32)
    return fold3(y2[:, 0:FIRST], y2[:, FIRST : 2 * FIRST], y2[:, 2 * FIRST :])


def multiply_points(left_t, right):
    left_limbs = [v.astype(jnp.bfloat16) for v in split3(left_t)]
    zero = jnp.zeros_like(left_limbs[0])
    cols = []
    for level in range(5):
        pieces = [left_limbs[level - y] if 0 <= level - y < 3 else zero for y in range(3)]
        cols.append(jnp.concatenate(pieces, axis=1))
    toeplitz = jnp.concatenate(cols, axis=2)
    right_limbs = limbs_bf16(right, 1)
    levels = jnp.einsum("pKa,pKj->paj", toeplitz, right_limbs, preferred_element_type=jnp.float32)
    n_i = left_t.shape[2]
    lv = [levels[:, n * n_i : (n + 1) * n_i] for n in range(5)]
    high = fold3(lv[2], lv[3], lv[4])
    return fold3(lv[0], lv[1], high)


def make_body(n_grp, n_pt, n_chunks):
    tables = build_tables()
    d_local = SECOND // n_pt

    def body(left_factor, right_factor):
        il, kl, _ = left_factor.shape
        jl = right_factor.shape[0]

        def to_points(x):
            rows = x.shape[0]
            xt = jnp.transpose(x, (2, 1, 0)).reshape(x.shape[2], kl * rows)
            ev = forward(xt, tables)
            ev = ev.reshape(FIRST, n_pt, d_local, kl, rows)
            ev = jnp.transpose(ev, (1, 0, 2, 3, 4))
            ev = lax.all_to_all(ev, "pt", split_axis=0, concat_axis=0, tiled=False)
            return ev

        left_pts = to_points(left_factor)
        left_pts = jnp.broadcast_to(left_pts[None], (n_grp,) + left_pts.shape)
        left_pts = lax.all_to_all(left_pts, "grp", split_axis=0, concat_axis=0, tiled=True)
        left_pts = jnp.transpose(left_pts, (2, 3, 1, 4, 0, 5))
        left_pts = left_pts.reshape(FIRST * d_local, n_pt * kl, n_grp * il)
        jc = jl // n_chunks
        prods = []
        for chunk in range(n_chunks):
            right_pts = to_points(right_factor[chunk * jc : (chunk + 1) * jc])
            right_pts = jnp.transpose(right_pts, (1, 2, 0, 3, 4)).reshape(FIRST * d_local, n_pt * kl, jc)
            prods.append(multiply_points(left_pts, right_pts))
        prod = jnp.concatenate(prods, axis=2) if n_chunks > 1 else prods[0]
        n_i = prod.shape[1]
        ib = n_i // n_grp
        jb = n_grp * jl // n_pt
        prod = prod.reshape(FIRST * d_local, n_grp, ib, jl)
        prod = lax.all_to_all(prod, "grp", split_axis=1, concat_axis=1, tiled=True)
        prod = jnp.transpose(prod, (0, 2, 1, 3)).reshape(FIRST, d_local, ib, n_pt, jb)
        prod = jnp.transpose(prod, (3, 0, 1, 2, 4))
        prod = lax.all_to_all(prod, "pt", split_axis=0, concat_axis=0, tiled=False)
        pv = jnp.transpose(prod, (0, 2, 1, 3, 4)).reshape(SECOND, FIRST, ib * jb)
        coeffs = inverse(pv, tables)
        coeffs = jnp.transpose(coeffs, (2, 1, 0)).reshape(ib, jb, LENGTH)
        return coeffs / float(modulus)

    return body


def solution(mesh):
    n_grp = mesh.shape["grp"]
    n_pt = mesh.shape["pt"]
    return jax.shard_map(
        make_body(n_grp, n_pt, 2),
        mesh=mesh,
        in_specs=(P("grp", "pt", None), P("grp", "pt", None)),
        out_specs=P("grp", "pt", None),
        check_vma=False,
    )
```

```python
import jax
import jax.numpy as jnp
import numpy as np
from jax import lax
from jax.sharding import PartitionSpec as P

FIRST = 32
SECOND = 128
HALF_FIRST = FIRST // 2
LENGTH = FIRST * SECOND

modulus = 7340033
INV_P = float(np.float32(1.0 / modulus))


def root_powers(length_all):
    for generator in range(2, 64):
        candidate = pow(generator, (modulus - 1) // length_all, modulus)
        if pow(candidate, length_all // 2, modulus) == modulus - 1:
            break
    powers = [1]
    for counter in range(length_all - 1):
        powers.append(powers[-1] * candidate % modulus)
    return np.array(powers, dtype=np.int64)


def balanced_limbs(values):
    v = np.asarray(values, dtype=np.int64)
    l0 = (v + 128) % 256 - 128
    v = (v - l0) // 256
    l1 = (v + 128) % 256 - 128
    l2 = (v - l1) // 256
    return [l0, l1, l2]


def scaled_stack(table):
    n, k = table.shape
    out = np.zeros((3, n, 3, k), dtype=np.float32)
    for level in range(3):
        scaled = table * pow(256, level, modulus) % modulus
        for limb, piece in enumerate(balanced_limbs(scaled)):
            out[limb, :, level, :] = piece
    return out.reshape(3 * n, 3 * k)


def twist_stack(table):
    out = np.zeros((3, 3) + table.shape, dtype=np.float32)
    for level in range(3):
        scaled = table * pow(256, level, modulus) % modulus
        for limb, piece in enumerate(balanced_limbs(scaled)):
            out[level, limb] = piece
    return out


def build_tables():
    powers = root_powers(LENGTH)

    def pw(e):
        return powers[np.asarray(e) % LENGTH]

    a16 = np.arange(HALF_FIRST)
    c32 = np.arange(FIRST)
    b128 = np.arange(SECOND)
    scale_inv = pow(LENGTH, modulus - 2, modulus)
    fwd1 = pw(SECOND * np.outer(c32, a16))
    fwd_twist = pw(np.outer(c32, b128))
    fwd2 = pw(FIRST * np.outer(b128, b128))
    inv1 = pw(-FIRST * np.outer(b128, b128))
    inv_twist = pw(-np.outer(c32, b128))
    inv2 = pw(-SECOND * np.outer(c32, c32)) * scale_inv % modulus
    return dict(
        fwd1=scaled_stack(fwd1),
        fwd_twist=twist_stack(fwd_twist),
        fwd2=scaled_stack(fwd2).T.copy(),
        inv1=scaled_stack(inv1).T.copy(),
        inv_twist=twist_stack(inv_twist),
        inv2=scaled_stack(inv2),
    )


def split3(x):
    h = jnp.floor(x * (1.0 / 256.0))
    x0 = x - 256.0 * h
    x2 = jnp.floor(h * (1.0 / 256.0))
    x1 = h - 256.0 * x2
    return x0, x1, x2


def fold3(s0, s1, s2):
    f = s2 * 65536.0 + s1 * 256.0 + s0
    q = jnp.round(f * INV_P)
    d = s2 - 112.0 * q
    e = s1 + 256.0 * d
    r = s0 + 256.0 * e - q
    return jnp.where(r < 0, r + float(modulus), r)


def twist(z, tw):
    zl = split3(z)
    s = [zl[0] * tw[0, u] + zl[1] * tw[1, u] + zl[2] * tw[2, u] for u in range(3)]
    return fold3(*s)


def limbs_bf16(x, axis):
    return jnp.concatenate([piece.astype(jnp.bfloat16) for piece in split3(x)], axis=axis)


def forward(x, tables):
    entries = x.shape[0]
    x = x.reshape(entries, HALF_FIRST, SECOND)
    xl = limbs_bf16(x, 1)
    y = jnp.einsum(
        "eLb,NL->eNb", xl, jnp.asarray(tables["fwd1"], jnp.bfloat16), preferred_element_type=jnp.float32
    )
    z = fold3(y[:, 0:FIRST], y[:, FIRST : 2 * FIRST], y[:, 2 * FIRST :])
    z = twist(z, jnp.asarray(tables["fwd_twist"]))
    zl = limbs_bf16(z, 2)
    y2 = jnp.einsum(
        "ecK,KN->Nec", zl, jnp.asarray(tables["fwd2"], jnp.bfloat16), preferred_element_type=jnp.float32
    )
    return fold3(y2[0:SECOND], y2[SECOND : 2 * SECOND], y2[2 * SECOND :])


def inverse(pv, tables):
    entries = pv.shape[0]
    pl_ = limbs_bf16(pv, 2)
    y = jnp.einsum(
        "ecK,KN->ecN", pl_, jnp.asarray(tables["inv1"], jnp.bfloat16), preferred_element_type=jnp.float32
    )
    z = fold3(y[..., 0:SECOND], y[..., SECOND : 2 * SECOND], y[..., 2 * SECOND :])
    z = twist(z, jnp.asarray(tables["inv_twist"]))
    zl = limbs_bf16(z, 1)
    y2 = jnp.einsum(
        "eLb,NL->eNb", zl, jnp.asarray(tables["inv2"], jnp.bfloat16), preferred_element_type=jnp.float32
    )
    out = fold3(y2[:, 0:FIRST], y2[:, FIRST : 2 * FIRST], y2[:, 2 * FIRST :])
    return out.reshape(entries, LENGTH)


def multiply_points(left, right):
    left_limbs = [v.astype(jnp.bfloat16) for v in split3(left)]
    zero = jnp.zeros_like(left_limbs[0])
    rows = []
    for level in range(5):
        pieces = [left_limbs[level - y] if 0 <= level - y < 3 else zero for y in range(3)]
        rows.append(jnp.concatenate(pieces, axis=2))
    toeplitz = jnp.concatenate(rows, axis=1)
    right_limbs = limbs_bf16(right, 2)
    levels = jnp.einsum("pak,pjk->paj", toeplitz, right_limbs, preferred_element_type=jnp.float32)
    n_i = left.shape[1]
    lv = [levels[:, n * n_i : (n + 1) * n_i] for n in range(5)]
    high = fold3(lv[2], lv[3], lv[4])
    return fold3(lv[0], lv[1], high)


def make_body(n_grp, n_pt, n_chunks):
    tables = build_tables()
    d_local = SECOND // n_pt

    def body(left_factor, right_factor):
        il, kl, _ = left_factor.shape
        jl = right_factor.shape[0]

        def to_points(x, rows):
            ev = forward(x.reshape(rows * kl, -1), tables)
            ev = ev.reshape(n_pt, d_local * rows * kl * FIRST // 128, 128)
            ev = lax.all_to_all(ev, "pt", split_axis=0, concat_axis=0, tiled=False)
            return ev.reshape(n_pt, d_local, rows, kl, FIRST)

        left_pts = to_points(left_factor, il)
        left_pts = jnp.broadcast_to(left_pts[None], (n_grp,) + left_pts.shape)
        left_pts = lax.all_to_all(left_pts, "grp", split_axis=0, concat_axis=0, tiled=True)
        left_pts = jnp.transpose(left_pts, (2, 5, 0, 3, 1, 4))
        left_pts = left_pts.reshape(d_local * FIRST, n_grp * il, n_pt * kl)
        jc = jl // n_chunks
        prods = []
        for chunk in range(n_chunks):
            right_pts = to_points(right_factor[chunk * jc : (chunk + 1) * jc], jc)
            right_pts = jnp.transpose(right_pts, (1, 4, 2, 0, 3)).reshape(d_local * FIRST, jc, n_pt * kl)
            prods.append(multiply_points(left_pts, right_pts))
        prod = jnp.concatenate(prods, axis=2) if n_chunks > 1 else prods[0]
        n_i = prod.shape[1]
        ib = n_i // n_grp
        jb = n_grp * jl // n_pt
        prod = prod.reshape(d_local * FIRST, n_grp, ib, jl)
        prod = lax.all_to_all(prod, "grp", split_axis=1, concat_axis=1, tiled=True)
        prod = jnp.transpose(prod, (0, 2, 1, 3)).reshape(d_local, FIRST, ib, n_pt, jb)
        prod = jnp.transpose(prod, (3, 0, 1, 2, 4))
        prod = lax.all_to_all(prod, "pt", split_axis=0, concat_axis=0, tiled=False)
        pv = jnp.transpose(prod, (3, 4, 2, 0, 1)).reshape(ib * jb, FIRST, SECOND)
        coeffs = inverse(pv, tables)
        return (coeffs / float(modulus)).reshape(ib, jb, LENGTH)

    return body


def solution(mesh):
    n_grp = mesh.shape["grp"]
    n_pt = mesh.shape["pt"]
    return jax.shard_map(
        make_body(n_grp, n_pt, 4),
        mesh=mesh,
        in_specs=(P("grp", "pt", None), P("grp", "pt", None)),
        out_specs=P("grp", "pt", None),
        check_vma=False,
    )
```

```python
import jax
import jax.numpy as jnp
import numpy as np
from jax import lax
from jax.sharding import PartitionSpec as P

FIRST = 32
SECOND = 128
HALF_FIRST = FIRST // 2
LENGTH = FIRST * SECOND

modulus = 7340033
INV_P = float(np.float32(1.0 / modulus))


def root_powers(length_all):
    for generator in range(2, 64):
        candidate = pow(generator, (modulus - 1) // length_all, modulus)
        if pow(candidate, length_all // 2, modulus) == modulus - 1:
            break
    powers = [1]
    for counter in range(length_all - 1):
        powers.append(powers[-1] * candidate % modulus)
    return np.array(powers, dtype=np.int64)


def balanced_limbs(values):
    v = np.asarray(values, dtype=np.int64)
    l0 = (v + 128) % 256 - 128
    v = (v - l0) // 256
    l1 = (v + 128) % 256 - 128
    l2 = (v - l1) // 256
    return [l0, l1, l2]


def scaled_stack(table):
    n, k = table.shape
    out = np.zeros((3, n, 3, k), dtype=np.float32)
    for level in range(3):
        scaled = table * pow(256, level, modulus) % modulus
        for limb, piece in enumerate(balanced_limbs(scaled)):
            out[limb, :, level, :] = piece
    return out.reshape(3 * n, 3 * k)


def twist_stack(table):
    out = np.zeros((3, 3) + table.shape, dtype=np.float32)
    for level in range(3):
        scaled = table * pow(256, level, modulus) % modulus
        for limb, piece in enumerate(balanced_limbs(scaled)):
            out[level, limb] = piece
    return out


def build_tables():
    powers = root_powers(LENGTH)

    def pw(e):
        return powers[np.asarray(e) % LENGTH]

    a16 = np.arange(HALF_FIRST)
    c32 = np.arange(FIRST)
    b128 = np.arange(SECOND)
    scale_inv = pow(LENGTH, modulus - 2, modulus)
    fwd1 = pw(SECOND * np.outer(c32, a16))
    fwd_twist = pw(np.outer(c32, b128))
    fwd2 = pw(FIRST * np.outer(b128, b128))
    inv1 = pw(-FIRST * np.outer(b128, b128))
    inv_twist = pw(-np.outer(c32, b128))
    inv2 = pw(-SECOND * np.outer(c32, c32)) * scale_inv % modulus
    return dict(
        fwd1=scaled_stack(fwd1),
        fwd_twist=twist_stack(fwd_twist),
        fwd2=scaled_stack(fwd2).T.copy(),
        inv1=scaled_stack(inv1).T.copy(),
        inv_twist=twist_stack(inv_twist),
        inv2=scaled_stack(inv2),
    )


def split3(x):
    h = jnp.floor(x * (1.0 / 256.0))
    x0 = x - 256.0 * h
    x2 = jnp.floor(h * (1.0 / 256.0))
    x1 = h - 256.0 * x2
    return x0, x1, x2


def fold3(s0, s1, s2):
    f = s2 * 65536.0 + s1 * 256.0 + s0
    q = jnp.round(f * INV_P)
    d = s2 - 112.0 * q
    e = s1 + 256.0 * d
    r = s0 + 256.0 * e - q
    return jnp.where(r < 0, r + float(modulus), r)


def twist(z, tw):
    zl = split3(z)
    s = [zl[0] * tw[0, u] + zl[1] * tw[1, u] + zl[2] * tw[2, u] for u in range(3)]
    return fold3(*s)


def limbs_bf16(x, axis):
    return jnp.concatenate([piece.astype(jnp.bfloat16) for piece in split3(x)], axis=axis)


def forward(x, tables):
    entries = x.shape[0]
    x = x.reshape(entries, HALF_FIRST, SECOND)
    xl = limbs_bf16(x, 1)
    y = jnp.einsum(
        "eLb,NL->eNb", xl, jnp.asarray(tables["fwd1"], jnp.bfloat16), preferred_element_type=jnp.float32
    )
    z = fold3(y[:, 0:FIRST], y[:, FIRST : 2 * FIRST], y[:, 2 * FIRST :])
    z = twist(z, jnp.asarray(tables["fwd_twist"]))
    zl = limbs_bf16(z, 2).reshape(entries * FIRST, 3 * SECOND)
    y2 = lax.dot_general(
        jnp.asarray(tables["fwd2"].T, jnp.bfloat16),
        zl,
        (((1,), (1,)), ((), ())),
        preferred_element_type=jnp.float32,
    )
    return fold3(y2[0:SECOND], y2[SECOND : 2 * SECOND], y2[2 * SECOND :])


def inverse(pv, tables):
    entries = pv.shape[0]
    pl_ = limbs_bf16(pv, 2)
    y = jnp.einsum(
        "ecK,KN->ecN", pl_, jnp.asarray(tables["inv1"], jnp.bfloat16), preferred_element_type=jnp.float32
    )
    z = fold3(y[..., 0:SECOND], y[..., SECOND : 2 * SECOND], y[..., 2 * SECOND :])
    z = twist(z, jnp.asarray(tables["inv_twist"]))
    zl = limbs_bf16(z, 1)
    y2 = jnp.einsum(
        "eLb,NL->eNb", zl, jnp.asarray(tables["inv2"], jnp.bfloat16), preferred_element_type=jnp.float32
    )
    out = fold3(y2[:, 0:FIRST], y2[:, FIRST : 2 * FIRST], y2[:, 2 * FIRST :])
    return out.reshape(entries, LENGTH)


def balanced3(x):
    h = jnp.floor((x + 128.0) * (1.0 / 256.0))
    x0 = x - 256.0 * h
    h2 = jnp.floor((h + 128.0) * (1.0 / 256.0))
    x1 = h - 256.0 * h2
    return x0, x1, h2


def multiply_points(left, right):
    x0, x1, x2 = split3(left)
    zero = jnp.zeros_like(left)
    scaled = [left, fold3(zero, x0, x1 + 256.0 * x2), fold3(zero, zero, left)]
    limbs = [balanced3(v) for v in scaled]
    rows = [jnp.concatenate([limbs[y][u].astype(jnp.bfloat16) for y in range(3)], axis=2) for u in range(3)]
    stacked = jnp.concatenate(rows, axis=1)
    right_limbs = limbs_bf16(right, 2)
    levels = jnp.einsum("pak,pjk->paj", stacked, right_limbs, preferred_element_type=jnp.float32)
    n_i = left.shape[1]
    return fold3(levels[:, 0:n_i], levels[:, n_i : 2 * n_i], levels[:, 2 * n_i :])


def make_body(n_grp, n_pt, n_chunks):
    tables = build_tables()
    d_local = SECOND // n_pt

    def body(left_factor, right_factor):
        il, kl, _ = left_factor.shape
        jl = right_factor.shape[0]

        def to_points(x, rows):
            ev = forward(x.reshape(rows * kl, -1), tables)
            ev = ev.reshape(n_pt, d_local, rows * kl * FIRST)
            ev = lax.all_to_all(ev, "pt", split_axis=0, concat_axis=0, tiled=False)
            return ev.reshape(n_pt, d_local, rows, kl, FIRST)

        left_pts = to_points(left_factor, il)
        left_pts = jnp.broadcast_to(left_pts[None], (n_grp,) + left_pts.shape)
        left_pts = lax.all_to_all(left_pts, "grp", split_axis=0, concat_axis=0, tiled=True)
        left_pts = jnp.transpose(left_pts, (2, 5, 0, 3, 1, 4))
        left_pts = left_pts.reshape(d_local * FIRST, n_grp * il, n_pt * kl)
        jc = jl // n_chunks
        prods = []
        for chunk in range(n_chunks):
            right_pts = to_points(right_factor[chunk * jc : (chunk + 1) * jc], jc)
            right_pts = jnp.transpose(right_pts, (1, 4, 2, 0, 3)).reshape(d_local * FIRST, jc, n_pt * kl)
            prods.append(multiply_points(left_pts, right_pts))
        prod = jnp.concatenate(prods, axis=2) if n_chunks > 1 else prods[0]
        n_i = prod.shape[1]
        ib = n_i // n_grp
        jb = n_grp * jl // n_pt
        prod = prod.reshape(d_local * FIRST, n_grp, ib, jl)
        prod = lax.all_to_all(prod, "grp", split_axis=1, concat_axis=1, tiled=True)
        prod = jnp.transpose(prod, (0, 2, 1, 3)).reshape(d_local, FIRST, ib, n_pt, jb)
        prod = jnp.transpose(prod, (3, 0, 1, 2, 4))
        prod = lax.all_to_all(prod, "pt", split_axis=0, concat_axis=0, tiled=False)
        pv = jnp.transpose(prod, (3, 4, 2, 0, 1)).reshape(ib * jb, FIRST, SECOND)
        coeffs = inverse(pv, tables)
        return (coeffs / float(modulus)).reshape(ib, jb, LENGTH)

    return body


def solution(mesh):
    n_grp = mesh.shape["grp"]
    n_pt = mesh.shape["pt"]
    return jax.shard_map(
        make_body(n_grp, n_pt, 4),
        mesh=mesh,
        in_specs=(P("grp", "pt", None), P("grp", "pt", None)),
        out_specs=P("grp", "pt", None),
        check_vma=False,
    )
```

```python
import jax
import jax.numpy as jnp
import numpy as np
from jax import lax
from jax.sharding import PartitionSpec as P

FIRST = 32
SECOND = 128
HALF_FIRST = FIRST // 2
LENGTH = FIRST * SECOND

modulus = 7340033
INV_P = float(np.float32(1.0 / modulus))


def root_powers(length_all):
    for generator in range(2, 64):
        candidate = pow(generator, (modulus - 1) // length_all, modulus)
        if pow(candidate, length_all // 2, modulus) == modulus - 1:
            break
    powers = [1]
    for counter in range(length_all - 1):
        powers.append(powers[-1] * candidate % modulus)
    return np.array(powers, dtype=np.int64)


def balanced_limbs(values):
    v = np.asarray(values, dtype=np.int64)
    l0 = (v + 128) % 256 - 128
    v = (v - l0) // 256
    l1 = (v + 128) % 256 - 128
    l2 = (v - l1) // 256
    return [l0, l1, l2]


def scaled_stack(table):
    n, k = table.shape
    out = np.zeros((3, n, 3, k), dtype=np.float32)
    for level in range(3):
        scaled = table * pow(256, level, modulus) % modulus
        for limb, piece in enumerate(balanced_limbs(scaled)):
            out[limb, :, level, :] = piece
    return out.reshape(3 * n, 3 * k)


def twist_stack(table):
    out = np.zeros((3, 3) + table.shape, dtype=np.float32)
    for level in range(3):
        scaled = table * pow(256, level, modulus) % modulus
        for limb, piece in enumerate(balanced_limbs(scaled)):
            out[level, limb] = piece
    return out


def build_tables():
    powers = root_powers(LENGTH)

    def pw(e):
        return powers[np.asarray(e) % LENGTH]

    a16 = np.arange(HALF_FIRST)
    c32 = np.arange(FIRST)
    b128 = np.arange(SECOND)
    scale_inv = pow(LENGTH, modulus - 2, modulus)
    fwd1 = pw(SECOND * np.outer(c32, a16))
    fwd_twist = pw(np.outer(c32, b128))
    fwd2 = pw(FIRST * np.outer(b128, b128))
    inv1 = pw(-FIRST * np.outer(b128, b128))
    inv_twist = pw(-np.outer(c32, b128))
    inv2 = pw(-SECOND * np.outer(c32, c32)) * scale_inv % modulus
    return dict(
        fwd1=scaled_stack(fwd1),
        fwd_twist=twist_stack(fwd_twist),
        fwd2=scaled_stack(fwd2).T.copy(),
        inv1=scaled_stack(inv1).T.copy(),
        inv_twist=twist_stack(inv_twist),
        inv2=scaled_stack(inv2),
    )


def split3(x):
    h = jnp.floor(x * (1.0 / 256.0))
    x0 = x - 256.0 * h
    x2 = jnp.floor(h * (1.0 / 256.0))
    x1 = h - 256.0 * x2
    return x0, x1, x2


def fold3(s0, s1, s2):
    f = s2 * 65536.0 + s1 * 256.0 + s0
    q = jnp.round(f * INV_P)
    d = s2 - 112.0 * q
    e = s1 + 256.0 * d
    r = s0 + 256.0 * e - q
    return jnp.where(r < 0, r + float(modulus), r)


def twist(z, tw):
    zl = split3(z)
    s = [zl[0] * tw[0, u] + zl[1] * tw[1, u] + zl[2] * tw[2, u] for u in range(3)]
    return fold3(*s)


def limbs_bf16(x, axis):
    return jnp.concatenate([piece.astype(jnp.bfloat16) for piece in split3(x)], axis=axis)


def forward(x, tables):
    entries = x.shape[0]
    x = x.reshape(entries, HALF_FIRST, SECOND)
    xl = limbs_bf16(x, 1)
    y = jnp.einsum(
        "eLb,NL->eNb", xl, jnp.asarray(tables["fwd1"], jnp.bfloat16), preferred_element_type=jnp.float32
    )
    z = fold3(y[:, 0:FIRST], y[:, FIRST : 2 * FIRST], y[:, 2 * FIRST :])
    z = twist(z, jnp.asarray(tables["fwd_twist"]))
    zl = limbs_bf16(z, 2).reshape(entries * FIRST, 3 * SECOND)
    y2 = lax.dot_general(
        jnp.asarray(tables["fwd2"].T, jnp.bfloat16),
        zl,
        (((1,), (1,)), ((), ())),
        preferred_element_type=jnp.float32,
    )
    return fold3(y2[0:SECOND], y2[SECOND : 2 * SECOND], y2[2 * SECOND :])


def inverse(pv, tables):
    entries = pv.shape[0]
    pl_ = limbs_bf16(pv, 2)
    y = jnp.einsum(
        "ecK,KN->ecN", pl_, jnp.asarray(tables["inv1"], jnp.bfloat16), preferred_element_type=jnp.float32
    )
    z = fold3(y[..., 0:SECOND], y[..., SECOND : 2 * SECOND], y[..., 2 * SECOND :])
    z = twist(z, jnp.asarray(tables["inv_twist"]))
    zl = limbs_bf16(z, 1)
    y2 = jnp.einsum(
        "eLb,NL->eNb", zl, jnp.asarray(tables["inv2"], jnp.bfloat16), preferred_element_type=jnp.float32
    )
    out = fold3(y2[:, 0:FIRST], y2[:, FIRST : 2 * FIRST], y2[:, 2 * FIRST :])
    return out.reshape(entries, LENGTH)


def balanced3(x):
    h = jnp.floor((x + 128.0) * (1.0 / 256.0))
    x0 = x - 256.0 * h
    h2 = jnp.floor((h + 128.0) * (1.0 / 256.0))
    x1 = h - 256.0 * h2
    return x0, x1, h2


def multiply_points(left, right):
    x0, x1, x2 = split3(left)
    zero = jnp.zeros_like(left)
    scaled = [left, fold3(zero, x0, x1 + 256.0 * x2), fold3(zero, zero, left)]
    limbs = [balanced3(v) for v in scaled]
    rows = [jnp.concatenate([limbs[y][u].astype(jnp.bfloat16) for y in range(3)], axis=2) for u in range(3)]
    stacked = jnp.concatenate(rows, axis=1)
    right_limbs = limbs_bf16(right, 2)
    levels = jnp.einsum("pak,pjk->paj", stacked, right_limbs, preferred_element_type=jnp.float32)
    n_i = left.shape[1]
    return fold3(levels[:, 0:n_i], levels[:, n_i : 2 * n_i], levels[:, 2 * n_i :])


def make_body(n_grp, n_pt, n_chunks):
    tables = build_tables()
    d_local = SECOND // n_pt

    def body(left_factor, right_factor):
        il, kl, _ = left_factor.shape
        jl = right_factor.shape[0]

        def to_points(x, rows):
            ev = forward(x.reshape(rows * kl, -1), tables)
            ev = ev.reshape(n_pt, d_local, rows * kl * FIRST)
            ev = lax.all_to_all(ev, "pt", split_axis=0, concat_axis=0, tiled=False)
            return ev.reshape(n_pt, d_local, rows, kl, FIRST)

        left_pts = to_points(left_factor, il)
        left_pts = lax.all_gather(left_pts, "grp", axis=0, tiled=False)
        left_pts = jnp.transpose(left_pts, (2, 5, 0, 3, 1, 4))
        left_pts = left_pts.reshape(d_local * FIRST, n_grp * il, n_pt * kl)
        jc = jl // n_chunks
        prods = []
        for chunk in range(n_chunks):
            right_pts = to_points(right_factor[chunk * jc : (chunk + 1) * jc], jc)
            right_pts = jnp.transpose(right_pts, (1, 4, 2, 0, 3)).reshape(d_local * FIRST, jc, n_pt * kl)
            prods.append(multiply_points(left_pts, right_pts))
        prod = jnp.concatenate(prods, axis=2) if n_chunks > 1 else prods[0]
        n_i = prod.shape[1]
        ib = n_i // n_grp
        jb = n_grp * jl // n_pt
        prod = prod.reshape(d_local * FIRST, n_grp, ib, jl)
        prod = lax.all_to_all(prod, "grp", split_axis=1, concat_axis=1, tiled=True)
        prod = jnp.transpose(prod, (0, 2, 1, 3)).reshape(d_local, FIRST, ib, n_pt, jb)
        prod = jnp.transpose(prod, (3, 0, 1, 2, 4))
        prod = lax.all_to_all(prod, "pt", split_axis=0, concat_axis=0, tiled=False)
        pv = jnp.transpose(prod, (3, 4, 2, 0, 1)).reshape(ib * jb, FIRST, SECOND)
        coeffs = inverse(pv, tables)
        return (coeffs / float(modulus)).reshape(ib, jb, LENGTH)

    return body


def solution(mesh):
    n_grp = mesh.shape["grp"]
    n_pt = mesh.shape["pt"]
    return jax.shard_map(
        make_body(n_grp, n_pt, 4),
        mesh=mesh,
        in_specs=(P("grp", "pt", None), P("grp", "pt", None)),
        out_specs=P("grp", "pt", None),
        check_vma=False,
    )
```

```python
import jax
import jax.numpy as jnp
import numpy as np
from jax import lax
from jax.sharding import PartitionSpec as P

FIRST = 32
SECOND = 128
HALF_FIRST = FIRST // 2
LENGTH = FIRST * SECOND

modulus = 7340033
INV_P = float(np.float32(1.0 / modulus))


def root_powers(length_all):
    for generator in range(2, 64):
        candidate = pow(generator, (modulus - 1) // length_all, modulus)
        if pow(candidate, length_all // 2, modulus) == modulus - 1:
            break
    powers = [1]
    for counter in range(length_all - 1):
        powers.append(powers[-1] * candidate % modulus)
    return np.array(powers, dtype=np.int64)


def balanced_limbs(values):
    v = np.asarray(values, dtype=np.int64)
    l0 = (v + 128) % 256 - 128
    v = (v - l0) // 256
    l1 = (v + 128) % 256 - 128
    l2 = (v - l1) // 256
    return [l0, l1, l2]


def scaled_stack(table):
    n, k = table.shape
    out = np.zeros((3, n, 3, k), dtype=np.float32)
    for level in range(3):
        scaled = table * pow(256, level, modulus) % modulus
        for limb, piece in enumerate(balanced_limbs(scaled)):
            out[limb, :, level, :] = piece
    return out.reshape(3 * n, 3 * k)


def twist_stack(table):
    out = np.zeros((3, 3) + table.shape, dtype=np.float32)
    for level in range(3):
        scaled = table * pow(256, level, modulus) % modulus
        for limb, piece in enumerate(balanced_limbs(scaled)):
            out[level, limb] = piece
    return out


def build_tables():
    powers = root_powers(LENGTH)

    def pw(e):
        return powers[np.asarray(e) % LENGTH]

    a16 = np.arange(HALF_FIRST)
    c32 = np.arange(FIRST)
    b128 = np.arange(SECOND)
    scale_inv = pow(LENGTH, modulus - 2, modulus)
    fwd1 = pw(SECOND * np.outer(c32, a16))
    fwd_twist = pw(np.outer(c32, b128))
    fwd2 = pw(FIRST * np.outer(b128, b128))
    inv1 = pw(-FIRST * np.outer(b128, b128))
    inv_twist = pw(-np.outer(c32, b128))
    inv2 = pw(-SECOND * np.outer(c32, c32)) * scale_inv % modulus
    return dict(
        fwd1=scaled_stack(fwd1),
        fwd_twist=twist_stack(fwd_twist),
        fwd2=scaled_stack(fwd2).T.copy(),
        inv1=scaled_stack(inv1).T.copy(),
        inv_twist=twist_stack(inv_twist),
        inv2=scaled_stack(inv2),
    )


def split3(x):
    h = jnp.floor(x * (1.0 / 256.0))
    x0 = x - 256.0 * h
    x2 = jnp.floor(h * (1.0 / 256.0))
    x1 = h - 256.0 * x2
    return x0, x1, x2


def fold3(s0, s1, s2):
    f = s2 * 65536.0 + s1 * 256.0 + s0
    q = jnp.round(f * INV_P)
    d = s2 - 112.0 * q
    e = s1 + 256.0 * d
    r = s0 + 256.0 * e - q
    return jnp.where(r < 0, r + float(modulus), r)


def twist(z, tw):
    zl = split3(z)
    s = [zl[0] * tw[0, u] + zl[1] * tw[1, u] + zl[2] * tw[2, u] for u in range(3)]
    return fold3(*s)


def limbs_bf16(x, axis):
    return jnp.concatenate([piece.astype(jnp.bfloat16) for piece in split3(x)], axis=axis)


def forward(x, tables):
    entries = x.shape[0]
    x = x.reshape(entries, HALF_FIRST, SECOND)
    xl = limbs_bf16(x, 1)
    y = jnp.einsum(
        "eLb,NL->eNb", xl, jnp.asarray(tables["fwd1"], jnp.bfloat16), preferred_element_type=jnp.float32
    )
    z = fold3(y[:, 0:FIRST], y[:, FIRST : 2 * FIRST], y[:, 2 * FIRST :])
    z = twist(z, jnp.asarray(tables["fwd_twist"]))
    zl = limbs_bf16(z, 2).reshape(entries * FIRST, 3 * SECOND)
    y2 = lax.dot_general(
        jnp.asarray(tables["fwd2"].T, jnp.bfloat16),
        zl,
        (((1,), (1,)), ((), ())),
        preferred_element_type=jnp.float32,
    )
    return fold3(y2[0:SECOND], y2[SECOND : 2 * SECOND], y2[2 * SECOND :])


def inverse(pv, tables):
    entries = pv.shape[0]
    pl_ = limbs_bf16(pv, 2)
    y = jnp.einsum(
        "ecK,KN->ecN", pl_, jnp.asarray(tables["inv1"], jnp.bfloat16), preferred_element_type=jnp.float32
    )
    z = fold3(y[..., 0:SECOND], y[..., SECOND : 2 * SECOND], y[..., 2 * SECOND :])
    z = twist(z, jnp.asarray(tables["inv_twist"]))
    zl = limbs_bf16(z, 1)
    y2 = jnp.einsum(
        "eLb,NL->eNb", zl, jnp.asarray(tables["inv2"], jnp.bfloat16), preferred_element_type=jnp.float32
    )
    out = fold3(y2[:, 0:FIRST], y2[:, FIRST : 2 * FIRST], y2[:, 2 * FIRST :])
    return out.reshape(entries, LENGTH)


def balanced3(x):
    h = jnp.floor((x + 128.0) * (1.0 / 256.0))
    x0 = x - 256.0 * h
    h2 = jnp.floor((h + 128.0) * (1.0 / 256.0))
    x1 = h - 256.0 * h2
    return x0, x1, h2


def multiply_points(left, right):
    x0, x1, x2 = split3(left)
    zero = jnp.zeros_like(left)
    scaled = [left, fold3(zero, x0, x1 + 256.0 * x2), fold3(zero, zero, left)]
    limbs = [balanced3(v) for v in scaled]
    rows = [jnp.concatenate([limbs[y][u].astype(jnp.bfloat16) for y in range(3)], axis=2) for u in range(3)]
    stacked = jnp.concatenate(rows, axis=1)
    right_limbs = limbs_bf16(right, 2)
    levels = jnp.einsum("pak,pjk->paj", stacked, right_limbs, preferred_element_type=jnp.float32)
    n_i = left.shape[1]
    return fold3(levels[:, 0:n_i], levels[:, n_i : 2 * n_i], levels[:, 2 * n_i :])


def make_body(n_grp, n_pt, n_chunks):
    tables = build_tables()
    d_local = SECOND // n_pt

    def body(left_factor, right_factor):
        il, kl, _ = left_factor.shape
        jl = right_factor.shape[0]

        def to_points(x, rows):
            ev = forward(x.reshape(rows * kl, -1), tables)
            ev = ev.reshape(n_pt, d_local, rows * kl * FIRST)
            ev = lax.all_to_all(ev, "pt", split_axis=0, concat_axis=0, tiled=False)
            return ev.reshape(n_pt, d_local, rows, kl, FIRST)

        left_pts = to_points(left_factor, il)
        left_pts = jnp.broadcast_to(left_pts[None], (n_grp,) + left_pts.shape)
        left_pts = lax.all_to_all(left_pts, "grp", split_axis=0, concat_axis=0, tiled=True)
        left_pts = jnp.transpose(left_pts, (2, 5, 0, 3, 1, 4))
        left_pts = left_pts.reshape(d_local * FIRST, n_grp * il, n_pt * kl)
        jc = jl // n_chunks
        prods = []
        for chunk in range(n_chunks):
            right_pts = to_points(right_factor[chunk * jc : (chunk + 1) * jc], jc)
            right_pts = jnp.transpose(right_pts, (1, 4, 2, 0, 3)).reshape(d_local * FIRST, jc, n_pt * kl)
            prods.append(multiply_points(left_pts, right_pts))
        prod = jnp.concatenate(prods, axis=2) if n_chunks > 1 else prods[0]
        n_i = prod.shape[1]
        ib = n_i // n_grp
        jb = n_grp * jl // n_pt
        prod = prod.reshape(d_local * FIRST, n_grp, ib, jl)
        prod = lax.all_to_all(prod, "grp", split_axis=1, concat_axis=1, tiled=True)
        prod = jnp.transpose(prod, (0, 2, 1, 3)).reshape(d_local, FIRST, ib, n_pt, jb)
        prod = jnp.transpose(prod, (3, 0, 1, 2, 4))
        prod = lax.all_to_all(prod, "pt", split_axis=0, concat_axis=0, tiled=False)
        pv = jnp.transpose(prod, (3, 4, 2, 0, 1)).reshape(ib * jb, FIRST, SECOND)
        coeffs = inverse(pv, tables)
        return (coeffs / float(modulus)).reshape(ib, jb, LENGTH)

    return body


def solution(mesh):
    n_grp = mesh.shape["grp"]
    n_pt = mesh.shape["pt"]
    return jax.shard_map(
        make_body(n_grp, n_pt, 8),
        mesh=mesh,
        in_specs=(P("grp", "pt", None), P("grp", "pt", None)),
        out_specs=P("grp", "pt", None),
        check_vma=False,
    )
```

```python
import jax
import jax.numpy as jnp
import numpy as np
from jax import lax
from jax.sharding import PartitionSpec as P

FIRST = 32
SECOND = 128
HALF_FIRST = FIRST // 2
LENGTH = FIRST * SECOND

modulus = 7340033
INV_P = float(np.float32(1.0 / modulus))


def root_powers(length_all):
    for generator in range(2, 64):
        candidate = pow(generator, (modulus - 1) // length_all, modulus)
        if pow(candidate, length_all // 2, modulus) == modulus - 1:
            break
    powers = [1]
    for counter in range(length_all - 1):
        powers.append(powers[-1] * candidate % modulus)
    return np.array(powers, dtype=np.int64)


def balanced_limbs(values):
    v = np.asarray(values, dtype=np.int64)
    l0 = (v + 128) % 256 - 128
    v = (v - l0) // 256
    l1 = (v + 128) % 256 - 128
    l2 = (v - l1) // 256
    return [l0, l1, l2]


def scaled_stack(table):
    n, k = table.shape
    out = np.zeros((3, n, 3, k), dtype=np.float32)
    for level in range(3):
        scaled = table * pow(256, level, modulus) % modulus
        for limb, piece in enumerate(balanced_limbs(scaled)):
            out[limb, :, level, :] = piece
    return out.reshape(3 * n, 3 * k)


def twist_stack(table):
    out = np.zeros((3, 3) + table.shape, dtype=np.float32)
    for level in range(3):
        scaled = table * pow(256, level, modulus) % modulus
        for limb, piece in enumerate(balanced_limbs(scaled)):
            out[level, limb] = piece
    return out


def build_tables():
    powers = root_powers(LENGTH)

    def pw(e):
        return powers[np.asarray(e) % LENGTH]

    a16 = np.arange(HALF_FIRST)
    c32 = np.arange(FIRST)
    b128 = np.arange(SECOND)
    scale_inv = pow(LENGTH, modulus - 2, modulus)
    fwd1 = pw(SECOND * np.outer(c32, a16))
    fwd_twist = pw(np.outer(c32, b128))
    fwd2 = pw(FIRST * np.outer(b128, b128))
    inv1 = pw(-FIRST * np.outer(b128, b128))
    inv_twist = pw(-np.outer(c32, b128))
    inv2 = pw(-SECOND * np.outer(c32, c32)) * scale_inv % modulus
    return dict(
        fwd1=scaled_stack(fwd1),
        fwd_twist=twist_stack(fwd_twist),
        fwd2=scaled_stack(fwd2).T.copy(),
        inv1=scaled_stack(inv1).T.copy(),
        inv_twist=twist_stack(inv_twist),
        inv2=scaled_stack(inv2),
    )


def split3(x):
    h = jnp.floor(x * (1.0 / 256.0))
    x0 = x - 256.0 * h
    x2 = jnp.floor(h * (1.0 / 256.0))
    x1 = h - 256.0 * x2
    return x0, x1, x2


def fold3(s0, s1, s2):
    f = s2 * 65536.0 + s1 * 256.0 + s0
    q = jnp.round(f * INV_P)
    d = s2 - 112.0 * q
    e = s1 + 256.0 * d
    r = s0 + 256.0 * e - q
    return jnp.where(r < 0, r + float(modulus), r)


def twist(z, tw):
    zl = split3(z)
    s = [zl[0] * tw[0, u] + zl[1] * tw[1, u] + zl[2] * tw[2, u] for u in range(3)]
    return fold3(*s)


def limbs_bf16(x, axis):
    return jnp.concatenate([piece.astype(jnp.bfloat16) for piece in split3(x)], axis=axis)


def forward(x, tables):
    entries = x.shape[0]
    x = x.reshape(entries, HALF_FIRST, SECOND)
    xl = limbs_bf16(x, 1)
    y = jnp.einsum(
        "eLb,NL->eNb", xl, jnp.asarray(tables["fwd1"], jnp.bfloat16), preferred_element_type=jnp.float32
    )
    z = fold3(y[:, 0:FIRST], y[:, FIRST : 2 * FIRST], y[:, 2 * FIRST :])
    z = twist(z, jnp.asarray(tables["fwd_twist"]))
    zl = limbs_bf16(z, 2).reshape(entries * FIRST, 3 * SECOND)
    y2 = lax.dot_general(
        jnp.asarray(tables["fwd2"].T, jnp.bfloat16),
        zl,
        (((1,), (1,)), ((), ())),
        preferred_element_type=jnp.float32,
    )
    return fold3(y2[0:SECOND], y2[SECOND : 2 * SECOND], y2[2 * SECOND :])


def inverse(pv, tables):
    entries = pv.shape[0]
    pl_ = limbs_bf16(pv, 2)
    y = jnp.einsum(
        "ecK,KN->ecN", pl_, jnp.asarray(tables["inv1"], jnp.bfloat16), preferred_element_type=jnp.float32
    )
    z = fold3(y[..., 0:SECOND], y[..., SECOND : 2 * SECOND], y[..., 2 * SECOND :])
    z = twist(z, jnp.asarray(tables["inv_twist"]))
    zl = limbs_bf16(z, 1)
    y2 = jnp.einsum(
        "eLb,NL->eNb", zl, jnp.asarray(tables["inv2"], jnp.bfloat16), preferred_element_type=jnp.float32
    )
    out = fold3(y2[:, 0:FIRST], y2[:, FIRST : 2 * FIRST], y2[:, 2 * FIRST :])
    return out.reshape(entries, LENGTH)


def balanced3(x):
    h = jnp.floor((x + 128.0) * (1.0 / 256.0))
    x0 = x - 256.0 * h
    h2 = jnp.floor((h + 128.0) * (1.0 / 256.0))
    x1 = h - 256.0 * h2
    return x0, x1, h2


def multiply_points(left, right):
    x0, x1, x2 = split3(left)
    zero = jnp.zeros_like(left)
    scaled = [left, fold3(zero, x0, x1 + 256.0 * x2), fold3(zero, zero, left)]
    limbs = [balanced3(v) for v in scaled]
    rows = [jnp.concatenate([limbs[y][u].astype(jnp.bfloat16) for y in range(3)], axis=2) for u in range(3)]
    stacked = jnp.concatenate(rows, axis=1)
    right_limbs = limbs_bf16(right, 2)
    levels = jnp.einsum("pak,pjk->paj", stacked, right_limbs, preferred_element_type=jnp.float32)
    n_i = left.shape[1]
    return fold3(levels[:, 0:n_i], levels[:, n_i : 2 * n_i], levels[:, 2 * n_i :])


def make_body(n_grp, n_pt, n_chunks):
    tables = build_tables()
    d_local = SECOND // n_pt

    def body(left_factor, right_factor):
        il, kl, _ = left_factor.shape
        jl = right_factor.shape[0]

        def to_points(x, rows):
            ev = forward(x.reshape(rows * kl, -1), tables)
            ev = ev.reshape(n_pt, d_local, rows * kl * FIRST)
            ev = lax.all_to_all(ev, "pt", split_axis=0, concat_axis=0, tiled=False)
            return ev.reshape(n_pt, d_local, rows, kl, FIRST)

        left_pts = to_points(left_factor, il)
        left_pts = jnp.broadcast_to(left_pts[None], (n_grp,) + left_pts.shape)
        left_pts = lax.all_to_all(left_pts, "grp", split_axis=0, concat_axis=0, tiled=True)
        left_pts = jnp.transpose(left_pts, (2, 5, 0, 3, 1, 4))
        left_pts = left_pts.reshape(d_local * FIRST, n_grp * il, n_pt * kl)
        jc = jl // n_chunks
        prods = []
        for chunk in range(n_chunks):
            right_pts = to_points(right_factor[chunk * jc : (chunk + 1) * jc], jc)
            right_pts = jnp.transpose(right_pts, (1, 4, 2, 0, 3)).reshape(d_local * FIRST, jc, n_pt * kl)
            prods.append(multiply_points(left_pts, right_pts))
        prod = jnp.concatenate(prods, axis=2) if n_chunks > 1 else prods[0]
        n_i = prod.shape[1]
        ib = n_i // n_grp
        jb = n_grp * jl // n_pt
        prod = prod.reshape(d_local * FIRST, n_grp, ib, jl)
        prod = lax.all_to_all(prod, "grp", split_axis=1, concat_axis=1, tiled=True)
        prod = jnp.transpose(prod, (0, 2, 1, 3)).reshape(d_local, FIRST, ib, n_pt, jb)
        prod = jnp.transpose(prod, (3, 0, 1, 2, 4))
        prod = lax.all_to_all(prod, "pt", split_axis=0, concat_axis=0, tiled=False)
        pv = jnp.transpose(prod, (3, 4, 2, 0, 1)).reshape(ib * jb, FIRST, SECOND)
        coeffs = inverse(pv, tables)
        return (coeffs / float(modulus)).reshape(ib, jb, LENGTH)

    return body


def solution(mesh):
    n_grp = mesh.shape["grp"]
    n_pt = mesh.shape["pt"]
    return jax.shard_map(
        make_body(n_grp, n_pt, 2),
        mesh=mesh,
        in_specs=(P("grp", "pt", None), P("grp", "pt", None)),
        out_specs=P("grp", "pt", None),
        check_vma=False,
    )
```

```python
import jax
import jax.numpy as jnp
import numpy as np
from jax import lax
from jax.sharding import PartitionSpec as P

FIRST = 32
SECOND = 128
HALF_FIRST = FIRST // 2
LENGTH = FIRST * SECOND

modulus = 7340033
INV_P = float(np.float32(1.0 / modulus))


def root_powers(length_all):
    for generator in range(2, 64):
        candidate = pow(generator, (modulus - 1) // length_all, modulus)
        if pow(candidate, length_all // 2, modulus) == modulus - 1:
            break
    powers = [1]
    for counter in range(length_all - 1):
        powers.append(powers[-1] * candidate % modulus)
    return np.array(powers, dtype=np.int64)


def balanced_limbs(values):
    v = np.asarray(values, dtype=np.int64)
    l0 = (v + 128) % 256 - 128
    v = (v - l0) // 256
    l1 = (v + 128) % 256 - 128
    l2 = (v - l1) // 256
    return [l0, l1, l2]


def scaled_stack(table):
    n, k = table.shape
    out = np.zeros((3, n, 3, k), dtype=np.float32)
    for level in range(3):
        scaled = table * pow(256, level, modulus) % modulus
        for limb, piece in enumerate(balanced_limbs(scaled)):
            out[limb, :, level, :] = piece
    return out.reshape(3 * n, 3 * k)


def twist_stack(table):
    out = np.zeros((3, 3) + table.shape, dtype=np.float32)
    for level in range(3):
        scaled = table * pow(256, level, modulus) % modulus
        for limb, piece in enumerate(balanced_limbs(scaled)):
            out[level, limb] = piece
    return out


def build_tables():
    powers = root_powers(LENGTH)

    def pw(e):
        return powers[np.asarray(e) % LENGTH]

    a16 = np.arange(HALF_FIRST)
    c32 = np.arange(FIRST)
    b128 = np.arange(SECOND)
    scale_inv = pow(LENGTH, modulus - 2, modulus)
    fwd1 = pw(SECOND * np.outer(c32, a16))
    fwd_twist = pw(np.outer(c32, b128))
    fwd2 = pw(FIRST * np.outer(b128, b128))
    inv1 = pw(-FIRST * np.outer(b128, b128))
    inv_twist = pw(-np.outer(c32, b128))
    inv2 = pw(-SECOND * np.outer(c32, c32)) * scale_inv % modulus
    return dict(
        fwd1=scaled_stack(fwd1),
        fwd_twist=twist_stack(fwd_twist),
        fwd2=scaled_stack(fwd2).T.copy(),
        inv1=scaled_stack(inv1).T.copy(),
        inv_twist=twist_stack(inv_twist),
        inv2=scaled_stack(inv2),
    )


def split3(x):
    h = jnp.floor(x * (1.0 / 256.0))
    x0 = x - 256.0 * h
    x2 = jnp.floor(h * (1.0 / 256.0))
    x1 = h - 256.0 * x2
    return x0, x1, x2


def fold3(s0, s1, s2):
    f = s2 * 65536.0 + s1 * 256.0 + s0
    q = jnp.round(f * INV_P)
    d = s2 - 112.0 * q
    e = s1 + 256.0 * d
    r = s0 + 256.0 * e - q
    return jnp.where(r < 0, r + float(modulus), r)


def twist(z, tw):
    zl = split3(z)
    s = [zl[0] * tw[0, u] + zl[1] * tw[1, u] + zl[2] * tw[2, u] for u in range(3)]
    return fold3(*s)


def limbs_bf16(x, axis):
    return jnp.concatenate([piece.astype(jnp.bfloat16) for piece in split3(x)], axis=axis)


def forward(x, tables):
    entries = x.shape[0]
    x = x.reshape(entries, HALF_FIRST, SECOND)
    xl = limbs_bf16(x, 1)
    y = jnp.einsum(
        "eLb,NL->eNb", xl, jnp.asarray(tables["fwd1"], jnp.bfloat16), preferred_element_type=jnp.float32
    )
    z = fold3(y[:, 0:FIRST], y[:, FIRST : 2 * FIRST], y[:, 2 * FIRST :])
    z = twist(z, jnp.asarray(tables["fwd_twist"]))
    zl = limbs_bf16(z, 2).reshape(entries * FIRST, 3 * SECOND)
    y2 = lax.dot_general(
        jnp.asarray(tables["fwd2"].T, jnp.bfloat16),
        zl,
        (((1,), (1,)), ((), ())),
        preferred_element_type=jnp.float32,
    )
    return fold3(y2[0:SECOND], y2[SECOND : 2 * SECOND], y2[2 * SECOND :])


def inverse(pv, tables):
    entries = pv.shape[0]
    pl_ = limbs_bf16(pv, 2)
    y = jnp.einsum(
        "ecK,KN->ecN", pl_, jnp.asarray(tables["inv1"], jnp.bfloat16), preferred_element_type=jnp.float32
    )
    z = fold3(y[..., 0:SECOND], y[..., SECOND : 2 * SECOND], y[..., 2 * SECOND :])
    z = twist(z, jnp.asarray(tables["inv_twist"]))
    zl = limbs_bf16(z, 1)
    y2 = jnp.einsum(
        "eLb,NL->eNb", zl, jnp.asarray(tables["inv2"], jnp.bfloat16), preferred_element_type=jnp.float32
    )
    out = fold3(y2[:, 0:FIRST], y2[:, FIRST : 2 * FIRST], y2[:, 2 * FIRST :])
    return out.reshape(entries, LENGTH)


def balanced3(x):
    h = jnp.floor((x + 128.0) * (1.0 / 256.0))
    x0 = x - 256.0 * h
    h2 = jnp.floor((h + 128.0) * (1.0 / 256.0))
    x1 = h - 256.0 * h2
    return x0, x1, h2


def multiply_points(left, right):
    x0, x1, x2 = split3(left)
    zero = jnp.zeros_like(left)
    scaled = [left, fold3(zero, x0, x1 + 256.0 * x2), fold3(zero, zero, left)]
    limbs = [balanced3(v) for v in scaled]
    rows = [jnp.concatenate([limbs[y][u].astype(jnp.bfloat16) for y in range(3)], axis=2) for u in range(3)]
    stacked = jnp.concatenate(rows, axis=1)
    right_limbs = limbs_bf16(right, 2)
    levels = jnp.einsum("pak,pjk->paj", stacked, right_limbs, preferred_element_type=jnp.float32)
    n_i = left.shape[1]
    return fold3(levels[:, 0:n_i], levels[:, n_i : 2 * n_i], levels[:, 2 * n_i :])


def make_body(n_grp, n_pt, n_chunks):
    tables = build_tables()
    d_local = SECOND // n_pt

    def body(left_factor, right_factor):
        il, kl, _ = left_factor.shape
        jl = right_factor.shape[0]

        def to_points(x, rows):
            ev = forward(x.reshape(rows * kl, -1), tables)
            ev = ev.reshape(n_pt, d_local, rows * kl * FIRST)
            ev = lax.all_to_all(ev, "pt", split_axis=0, concat_axis=0, tiled=False)
            return ev.reshape(n_pt, d_local, rows, kl, FIRST)

        left_all = lax.all_gather(left_factor, "grp", axis=0, tiled=True)
        n_i = left_all.shape[0]
        jc = jl // n_chunks
        left_pts = None
        prods = []
        for chunk in range(n_chunks):
            right_part = right_factor[chunk * jc : (chunk + 1) * jc]
            if chunk == 0:
                both = to_points(jnp.concatenate([left_all, right_part], axis=0), n_i + jc)
                left_pts = jnp.transpose(both[:, :, :n_i], (1, 4, 2, 0, 3))
                left_pts = left_pts.reshape(d_local * FIRST, n_i, n_pt * kl)
                right_pts = both[:, :, n_i:]
            else:
                right_pts = to_points(right_part, jc)
            right_pts = jnp.transpose(right_pts, (1, 4, 2, 0, 3)).reshape(d_local * FIRST, jc, n_pt * kl)
            prods.append(multiply_points(left_pts, right_pts))
        prod = jnp.concatenate(prods, axis=2) if n_chunks > 1 else prods[0]
        ib = n_i // n_grp
        jb = n_grp * jl // n_pt
        prod = prod.reshape(d_local * FIRST, n_grp, ib, jl)
        prod = lax.all_to_all(prod, "grp", split_axis=1, concat_axis=1, tiled=True)
        prod = jnp.transpose(prod, (0, 2, 1, 3)).reshape(d_local, FIRST, ib, n_pt, jb)
        prod = jnp.transpose(prod, (3, 0, 1, 2, 4))
        prod = lax.all_to_all(prod, "pt", split_axis=0, concat_axis=0, tiled=False)
        pv = jnp.transpose(prod, (3, 4, 2, 0, 1)).reshape(ib * jb, FIRST, SECOND)
        coeffs = inverse(pv, tables)
        return (coeffs / float(modulus)).reshape(ib, jb, LENGTH)

    return body


def solution(mesh):
    n_grp = mesh.shape["grp"]
    n_pt = mesh.shape["pt"]
    return jax.shard_map(
        make_body(n_grp, n_pt, 2),
        mesh=mesh,
        in_specs=(P("grp", "pt", None), P("grp", "pt", None)),
        out_specs=P("grp", "pt", None),
        check_vma=False,
    )
```

```python
import jax
import jax.numpy as jnp
import numpy as np
from jax import lax
from jax.sharding import PartitionSpec as P

FIRST = 32
SECOND = 128
HALF_FIRST = FIRST // 2
LENGTH = FIRST * SECOND

modulus = 7340033
INV_P = float(np.float32(1.0 / modulus))


def root_powers(length_all):
    for generator in range(2, 64):
        candidate = pow(generator, (modulus - 1) // length_all, modulus)
        if pow(candidate, length_all // 2, modulus) == modulus - 1:
            break
    powers = [1]
    for counter in range(length_all - 1):
        powers.append(powers[-1] * candidate % modulus)
    return np.array(powers, dtype=np.int64)


def balanced_limbs(values):
    v = np.asarray(values, dtype=np.int64)
    l0 = (v + 128) % 256 - 128
    v = (v - l0) // 256
    l1 = (v + 128) % 256 - 128
    l2 = (v - l1) // 256
    return [l0, l1, l2]


def scaled_stack(table):
    n, k = table.shape
    out = np.zeros((3, n, 3, k), dtype=np.float32)
    for level in range(3):
        scaled = table * pow(256, level, modulus) % modulus
        for limb, piece in enumerate(balanced_limbs(scaled)):
            out[limb, :, level, :] = piece
    return out.reshape(3 * n, 3 * k)


def twist_stack(table):
    out = np.zeros((3, 3) + table.shape, dtype=np.float32)
    for level in range(3):
        scaled = table * pow(256, level, modulus) % modulus
        for limb, piece in enumerate(balanced_limbs(scaled)):
            out[level, limb] = piece
    return out


def build_tables():
    powers = root_powers(LENGTH)

    def pw(e):
        return powers[np.asarray(e) % LENGTH]

    a16 = np.arange(HALF_FIRST)
    c32 = np.arange(FIRST)
    b128 = np.arange(SECOND)
    scale_inv = pow(LENGTH, modulus - 2, modulus)
    fwd1 = pw(SECOND * np.outer(c32, a16))
    fwd_twist = pw(np.outer(c32, b128))
    fwd2 = pw(FIRST * np.outer(b128, b128))
    inv1 = pw(-FIRST * np.outer(b128, b128))
    inv_twist = pw(-np.outer(c32, b128))
    inv2 = pw(-SECOND * np.outer(c32, c32)) * scale_inv % modulus
    return dict(
        fwd1=scaled_stack(fwd1),
        fwd_twist=twist_stack(fwd_twist),
        fwd2=scaled_stack(fwd2).T.copy(),
        inv1=scaled_stack(inv1).T.copy(),
        inv_twist=twist_stack(inv_twist),
        inv2=scaled_stack(inv2),
    )


def split3(x):
    h = jnp.floor(x * (1.0 / 256.0))
    x0 = x - 256.0 * h
    x2 = jnp.floor(h * (1.0 / 256.0))
    x1 = h - 256.0 * x2
    return x0, x1, x2


def fold3(s0, s1, s2):
    f = s2 * 65536.0 + s1 * 256.0 + s0
    q = jnp.round(f * INV_P)
    d = s2 - 112.0 * q
    e = s1 + 256.0 * d
    r = s0 + 256.0 * e - q
    return jnp.where(r < 0, r + float(modulus), r)


def twist(z, tw):
    zl = split3(z)
    s = [zl[0] * tw[0, u] + zl[1] * tw[1, u] + zl[2] * tw[2, u] for u in range(3)]
    return fold3(*s)


def limbs_bf16(x, axis):
    return jnp.concatenate([piece.astype(jnp.bfloat16) for piece in split3(x)], axis=axis)


def forward(x, tables):
    entries = x.shape[0]
    x = x.reshape(entries, HALF_FIRST, SECOND)
    xl = limbs_bf16(x, 1)
    y = jnp.einsum(
        "eLb,NL->eNb", xl, jnp.asarray(tables["fwd1"], jnp.bfloat16), preferred_element_type=jnp.float32
    )
    z = fold3(y[:, 0:FIRST], y[:, FIRST : 2 * FIRST], y[:, 2 * FIRST :])
    z = twist(z, jnp.asarray(tables["fwd_twist"]))
    zl = limbs_bf16(z, 2).reshape(entries * FIRST, 3 * SECOND)
    y2 = lax.dot_general(
        jnp.asarray(tables["fwd2"].T, jnp.bfloat16),
        zl,
        (((1,), (1,)), ((), ())),
        preferred_element_type=jnp.float32,
    )
    return fold3(y2[0:SECOND], y2[SECOND : 2 * SECOND], y2[2 * SECOND :])


def inverse(pv, tables):
    entries = pv.shape[0]
    pl_ = limbs_bf16(pv, 2)
    y = jnp.einsum(
        "ecK,KN->ecN", pl_, jnp.asarray(tables["inv1"], jnp.bfloat16), preferred_element_type=jnp.float32
    )
    z = fold3(y[..., 0:SECOND], y[..., SECOND : 2 * SECOND], y[..., 2 * SECOND :])
    z = twist(z, jnp.asarray(tables["inv_twist"]))
    zl = limbs_bf16(z, 1)
    y2 = jnp.einsum(
        "eLb,NL->eNb", zl, jnp.asarray(tables["inv2"], jnp.bfloat16), preferred_element_type=jnp.float32
    )
    out = fold3(y2[:, 0:FIRST], y2[:, FIRST : 2 * FIRST], y2[:, 2 * FIRST :])
    return out.reshape(entries, LENGTH)


def balanced3(x):
    h = jnp.floor((x + 128.0) * (1.0 / 256.0))
    x0 = x - 256.0 * h
    h2 = jnp.floor((h + 128.0) * (1.0 / 256.0))
    x1 = h - 256.0 * h2
    return x0, x1, h2


def multiply_points(left, right):
    x0, x1, x2 = split3(left)
    zero = jnp.zeros_like(left)
    scaled = [left, fold3(zero, x0, x1 + 256.0 * x2), fold3(zero, zero, left)]
    limbs = [balanced3(v) for v in scaled]
    rows = [jnp.concatenate([limbs[y][u].astype(jnp.bfloat16) for y in range(3)], axis=2) for u in range(3)]
    stacked = jnp.concatenate(rows, axis=1)
    right_limbs = limbs_bf16(right, 2)
    levels = jnp.einsum("pak,pjk->paj", stacked, right_limbs, preferred_element_type=jnp.float32)
    n_i = left.shape[1]
    return fold3(levels[:, 0:n_i], levels[:, n_i : 2 * n_i], levels[:, 2 * n_i :])


def make_body(n_grp, n_pt, n_chunks):
    tables = build_tables()
    d_local = SECOND // n_pt

    def body(left_factor, right_factor):
        il, kl, _ = left_factor.shape
        jl = right_factor.shape[0]

        def send_points(x, rows):
            ev = forward(x.reshape(rows * kl, -1), tables)
            return ev.reshape(n_pt, d_local, rows * kl * FIRST)

        def exchange(ev):
            return lax.all_to_all(ev, "pt", split_axis=0, concat_axis=0, tiled=False)

        left_all = lax.all_gather(left_factor, "grp", axis=0, tiled=True)
        n_i = left_all.shape[0]
        jc = jl // n_chunks
        sends = []
        for chunk in range(n_chunks):
            right_part = right_factor[chunk * jc : (chunk + 1) * jc]
            if chunk == 0:
                right_part = jnp.concatenate([left_all, right_part], axis=0)
            sends.append(send_points(right_part, right_part.shape[0]))
        received = exchange(sends[0])
        left_pts = None
        prods = []
        for chunk in range(n_chunks):
            if chunk + 1 < n_chunks:
                received, sends[chunk + 1] = lax.optimization_barrier((received, sends[chunk + 1]))
                nxt = exchange(sends[chunk + 1])
            rows = received.shape[2] // (kl * FIRST)
            both = received.reshape(n_pt, d_local, rows, kl, FIRST)
            if chunk == 0:
                left_pts = jnp.transpose(both[:, :, :n_i], (1, 4, 2, 0, 3))
                left_pts = left_pts.reshape(d_local * FIRST, n_i, n_pt * kl)
                right_pts = both[:, :, n_i:]
            else:
                right_pts = both
            right_pts = jnp.transpose(right_pts, (1, 4, 2, 0, 3)).reshape(d_local * FIRST, jc, n_pt * kl)
            prods.append(multiply_points(left_pts, right_pts))
            if chunk + 1 < n_chunks:
                received = nxt
        prod = jnp.concatenate(prods, axis=2) if n_chunks > 1 else prods[0]
        ib = n_i // n_grp
        jb = n_grp * jl // n_pt
        prod = prod.reshape(d_local * FIRST, n_grp, ib, jl)
        prod = lax.all_to_all(prod, "grp", split_axis=1, concat_axis=1, tiled=True)
        prod = jnp.transpose(prod, (0, 2, 1, 3)).reshape(d_local, FIRST, ib, n_pt, jb)
        prod = jnp.transpose(prod, (3, 0, 1, 2, 4))
        prod = lax.all_to_all(prod, "pt", split_axis=0, concat_axis=0, tiled=False)
        pv = jnp.transpose(prod, (3, 4, 2, 0, 1)).reshape(ib * jb, FIRST, SECOND)
        coeffs = inverse(pv, tables)
        return (coeffs / float(modulus)).reshape(ib, jb, LENGTH)

    return body


def solution(mesh):
    n_grp = mesh.shape["grp"]
    n_pt = mesh.shape["pt"]
    return jax.shard_map(
        make_body(n_grp, n_pt, 2),
        mesh=mesh,
        in_specs=(P("grp", "pt", None), P("grp", "pt", None)),
        out_specs=P("grp", "pt", None),
        check_vma=False,
    )
```

```python
import jax
import jax.numpy as jnp
import numpy as np
from jax import lax
from jax.sharding import PartitionSpec as P

FIRST = 32
SECOND = 128
HALF_FIRST = FIRST // 2
LENGTH = FIRST * SECOND

modulus = 7340033
INV_P = float(np.float32(1.0 / modulus))


def root_powers(length_all):
    for generator in range(2, 64):
        candidate = pow(generator, (modulus - 1) // length_all, modulus)
        if pow(candidate, length_all // 2, modulus) == modulus - 1:
            break
    powers = [1]
    for counter in range(length_all - 1):
        powers.append(powers[-1] * candidate % modulus)
    return np.array(powers, dtype=np.int64)


def balanced_limbs(values):
    v = np.asarray(values, dtype=np.int64)
    l0 = (v + 128) % 256 - 128
    v = (v - l0) // 256
    l1 = (v + 128) % 256 - 128
    l2 = (v - l1) // 256
    return [l0, l1, l2]


def scaled_stack(table):
    n, k = table.shape
    out = np.zeros((3, n, 3, k), dtype=np.float32)
    for level in range(3):
        scaled = table * pow(256, level, modulus) % modulus
        for limb, piece in enumerate(balanced_limbs(scaled)):
            out[limb, :, level, :] = piece
    return out.reshape(3 * n, 3 * k)


def twist_stack(table):
    out = np.zeros((3, 3) + table.shape, dtype=np.float32)
    for level in range(3):
        scaled = table * pow(256, level, modulus) % modulus
        for limb, piece in enumerate(balanced_limbs(scaled)):
            out[level, limb] = piece
    return out


def build_tables():
    powers = root_powers(LENGTH)

    def pw(e):
        return powers[np.asarray(e) % LENGTH]

    a16 = np.arange(HALF_FIRST)
    c32 = np.arange(FIRST)
    b128 = np.arange(SECOND)
    scale_inv = pow(LENGTH, modulus - 2, modulus)
    fwd1 = pw(SECOND * np.outer(c32, a16))
    fwd_twist = pw(np.outer(c32, b128))
    fwd2 = pw(FIRST * np.outer(b128, b128))
    inv1 = pw(-FIRST * np.outer(b128, b128))
    inv_twist = pw(-np.outer(c32, b128))
    inv2 = pw(-SECOND * np.outer(c32, c32)) * scale_inv % modulus
    return dict(
        fwd1=scaled_stack(fwd1),
        fwd_twist=twist_stack(fwd_twist),
        fwd2=scaled_stack(fwd2).T.copy(),
        inv1=scaled_stack(inv1).T.copy(),
        inv_twist=twist_stack(inv_twist),
        inv2=scaled_stack(inv2),
    )


def split3(x):
    h = jnp.floor(x * (1.0 / 256.0))
    x0 = x - 256.0 * h
    x2 = jnp.floor(h * (1.0 / 256.0))
    x1 = h - 256.0 * x2
    return x0, x1, x2


def fold3(s0, s1, s2):
    f = s2 * 65536.0 + s1 * 256.0 + s0
    q = jnp.round(f * INV_P)
    d = s2 - 112.0 * q
    e = s1 + 256.0 * d
    r = s0 + 256.0 * e - q
    return jnp.where(r < 0, r + float(modulus), r)


def twist(z, tw):
    zl = split3(z)
    s = [zl[0] * tw[0, u] + zl[1] * tw[1, u] + zl[2] * tw[2, u] for u in range(3)]
    return fold3(*s)


def limbs_bf16(x, axis):
    return jnp.concatenate([piece.astype(jnp.bfloat16) for piece in split3(x)], axis=axis)


def forward(x, tables):
    entries = x.shape[0]
    x = x.reshape(entries, HALF_FIRST, SECOND)
    xl = limbs_bf16(x, 1)
    y = jnp.einsum(
        "eLb,NL->eNb", xl, jnp.asarray(tables["fwd1"], jnp.bfloat16), preferred_element_type=jnp.float32
    )
    z = fold3(y[:, 0:FIRST], y[:, FIRST : 2 * FIRST], y[:, 2 * FIRST :])
    z = twist(z, jnp.asarray(tables["fwd_twist"]))
    zl = limbs_bf16(z, 2).reshape(entries * FIRST, 3 * SECOND)
    y2 = lax.dot_general(
        jnp.asarray(tables["fwd2"].T, jnp.bfloat16),
        zl,
        (((1,), (1,)), ((), ())),
        preferred_element_type=jnp.float32,
    )
    return fold3(y2[0:SECOND], y2[SECOND : 2 * SECOND], y2[2 * SECOND :])


def inverse(pv, tables):
    entries = pv.shape[0]
    pl_ = limbs_bf16(pv, 2)
    y = jnp.einsum(
        "ecK,KN->ecN", pl_, jnp.asarray(tables["inv1"], jnp.bfloat16), preferred_element_type=jnp.float32
    )
    z = fold3(y[..., 0:SECOND], y[..., SECOND : 2 * SECOND], y[..., 2 * SECOND :])
    z = twist(z, jnp.asarray(tables["inv_twist"]))
    zl = limbs_bf16(z, 1)
    y2 = jnp.einsum(
        "eLb,NL->eNb", zl, jnp.asarray(tables["inv2"], jnp.bfloat16), preferred_element_type=jnp.float32
    )
    out = fold3(y2[:, 0:FIRST], y2[:, FIRST : 2 * FIRST], y2[:, 2 * FIRST :])
    return out.reshape(entries, LENGTH)


def balanced3(x):
    h = jnp.floor((x + 128.0) * (1.0 / 256.0))
    x0 = x - 256.0 * h
    h2 = jnp.floor((h + 128.0) * (1.0 / 256.0))
    x1 = h - 256.0 * h2
    return x0, x1, h2


def multiply_points(left, right):
    x0, x1, x2 = split3(left)
    zero = jnp.zeros_like(left)
    scaled = [left, fold3(zero, x0, x1 + 256.0 * x2), fold3(zero, zero, left)]
    limbs = [balanced3(v) for v in scaled]
    rows = [jnp.concatenate([limbs[y][u].astype(jnp.bfloat16) for y in range(3)], axis=2) for u in range(3)]
    stacked = jnp.concatenate(rows, axis=1)
    right_limbs = limbs_bf16(right, 2)
    levels = jnp.einsum("pak,pjk->paj", stacked, right_limbs, preferred_element_type=jnp.float32)
    n_i = left.shape[1]
    return fold3(levels[:, 0:n_i], levels[:, n_i : 2 * n_i], levels[:, 2 * n_i :])


def make_body(n_grp, n_pt):
    tables = build_tables()
    d_local = SECOND // n_pt

    def body(left_factor, right_factor):
        il, kl, _ = left_factor.shape
        jl = right_factor.shape[0]

        def send_points(x, rows):
            ev = forward(x.reshape(rows * kl, -1), tables)
            return ev.reshape(n_pt, d_local, rows * kl * FIRST)

        def exchange(ev):
            return lax.all_to_all(ev, "pt", split_axis=0, concat_axis=0, tiled=False)

        left_all = lax.all_gather(left_factor, "grp", axis=0, tiled=True)
        n_i = left_all.shape[0]
        sizes = [jl // 2, 3 * jl // 8, jl - jl // 2 - 3 * jl // 8] if jl % 8 == 0 else [jl]
        sizes = [size for size in sizes if size > 0]
        n_chunks = len(sizes)
        offsets = [sum(sizes[:chunk]) for chunk in range(n_chunks)]
        sends = []
        for chunk in range(n_chunks):
            right_part = right_factor[offsets[chunk] : offsets[chunk] + sizes[chunk]]
            if chunk == 0:
                right_part = jnp.concatenate([left_all, right_part], axis=0)
            sends.append(send_points(right_part, right_part.shape[0]))
        received = exchange(sends[0])
        left_pts = None
        prods = []
        for chunk in range(n_chunks):
            if chunk + 1 < n_chunks:
                received, sends[chunk + 1] = lax.optimization_barrier((received, sends[chunk + 1]))
                nxt = exchange(sends[chunk + 1])
            rows = received.shape[2] // (kl * FIRST)
            both = received.reshape(n_pt, d_local, rows, kl, FIRST)
            if chunk == 0:
                left_pts = jnp.transpose(both[:, :, :n_i], (1, 4, 2, 0, 3))
                left_pts = left_pts.reshape(d_local * FIRST, n_i, n_pt * kl)
                right_pts = both[:, :, n_i:]
            else:
                right_pts = both
            right_pts = jnp.transpose(right_pts, (1, 4, 2, 0, 3)).reshape(d_local * FIRST, sizes[chunk], n_pt * kl)
            prods.append(multiply_points(left_pts, right_pts))
            if chunk + 1 < n_chunks:
                received = nxt
        prod = jnp.concatenate(prods, axis=2) if n_chunks > 1 else prods[0]
        ib = n_i // n_grp
        jb = n_grp * jl // n_pt
        prod = prod.reshape(d_local * FIRST, n_grp, ib, jl)
        prod = lax.all_to_all(prod, "grp", split_axis=1, concat_axis=1, tiled=True)
        prod = jnp.transpose(prod, (0, 2, 1, 3)).reshape(d_local, FIRST, ib, n_pt, jb)
        prod = jnp.transpose(prod, (3, 0, 1, 2, 4))
        prod = lax.all_to_all(prod, "pt", split_axis=0, concat_axis=0, tiled=False)
        pv = jnp.transpose(prod, (3, 4, 2, 0, 1)).reshape(ib * jb, FIRST, SECOND)
        coeffs = inverse(pv, tables)
        return (coeffs / float(modulus)).reshape(ib, jb, LENGTH)

    return body


def solution(mesh):
    n_grp = mesh.shape["grp"]
    n_pt = mesh.shape["pt"]
    return jax.shard_map(
        make_body(n_grp, n_pt),
        mesh=mesh,
        in_specs=(P("grp", "pt", None), P("grp", "pt", None)),
        out_specs=P("grp", "pt", None),
        check_vma=False,
    )
```

```python
import jax
import jax.numpy as jnp
import numpy as np
from jax import lax
from jax.sharding import PartitionSpec as P

FIRST = 32
SECOND = 128
HALF_FIRST = FIRST // 2
LENGTH = FIRST * SECOND

modulus = 7340033
INV_P = float(np.float32(1.0 / modulus))


def root_powers(length_all):
    for generator in range(2, 64):
        candidate = pow(generator, (modulus - 1) // length_all, modulus)
        if pow(candidate, length_all // 2, modulus) == modulus - 1:
            break
    powers = [1]
    for counter in range(length_all - 1):
        powers.append(powers[-1] * candidate % modulus)
    return np.array(powers, dtype=np.int64)


def balanced_limbs(values):
    v = np.asarray(values, dtype=np.int64)
    l0 = (v + 128) % 256 - 128
    v = (v - l0) // 256
    l1 = (v + 128) % 256 - 128
    l2 = (v - l1) // 256
    return [l0, l1, l2]


def scaled_stack(table):
    n, k = table.shape
    out = np.zeros((3, n, 3, k), dtype=np.float32)
    for level in range(3):
        scaled = table * pow(256, level, modulus) % modulus
        for limb, piece in enumerate(balanced_limbs(scaled)):
            out[limb, :, level, :] = piece
    return out.reshape(3 * n, 3 * k)


def twist_stack(table):
    out = np.zeros((3, 3) + table.shape, dtype=np.float32)
    for level in range(3):
        scaled = table * pow(256, level, modulus) % modulus
        for limb, piece in enumerate(balanced_limbs(scaled)):
            out[level, limb] = piece
    return out


def build_tables():
    powers = root_powers(LENGTH)

    def pw(e):
        return powers[np.asarray(e) % LENGTH]

    a16 = np.arange(HALF_FIRST)
    c32 = np.arange(FIRST)
    b128 = np.arange(SECOND)
    scale_inv = pow(LENGTH, modulus - 2, modulus)
    fwd1 = pw(SECOND * np.outer(c32, a16))
    fwd_twist = pw(np.outer(c32, b128))
    fwd2 = pw(FIRST * np.outer(b128, b128))
    inv1 = pw(-FIRST * np.outer(b128, b128))
    inv_twist = pw(-np.outer(c32, b128))
    inv2 = pw(-SECOND * np.outer(c32, c32)) * scale_inv % modulus
    return dict(
        fwd1=scaled_stack(fwd1),
        fwd_twist=twist_stack(fwd_twist),
        fwd2=scaled_stack(fwd2).T.copy(),
        inv1=scaled_stack(inv1).T.copy(),
        inv_twist=twist_stack(inv_twist),
        inv2=scaled_stack(inv2),
    )


def split3(x):
    h = jnp.floor(x * (1.0 / 256.0))
    x0 = x - 256.0 * h
    x2 = jnp.floor(h * (1.0 / 256.0))
    x1 = h - 256.0 * x2
    return x0, x1, x2


def fold3(s0, s1, s2):
    f = s2 * 65536.0 + s1 * 256.0 + s0
    q = jnp.round(f * INV_P)
    d = s2 - 112.0 * q
    e = s1 + 256.0 * d
    r = s0 + 256.0 * e - q
    return jnp.where(r < 0, r + float(modulus), r)


def twist(z, tw):
    zl = split3(z)
    s = [zl[0] * tw[0, u] + zl[1] * tw[1, u] + zl[2] * tw[2, u] for u in range(3)]
    return fold3(*s)


def limbs_bf16(x, axis):
    return jnp.concatenate([piece.astype(jnp.bfloat16) for piece in split3(x)], axis=axis)


def forward(x, tables):
    entries = x.shape[0]
    x = x.reshape(entries, HALF_FIRST, SECOND)
    xl = limbs_bf16(x, 1)
    y = jnp.einsum(
        "eLb,NL->eNb", xl, jnp.asarray(tables["fwd1"], jnp.bfloat16), preferred_element_type=jnp.float32
    )
    z = fold3(y[:, 0:FIRST], y[:, FIRST : 2 * FIRST], y[:, 2 * FIRST :])
    z = twist(z, jnp.asarray(tables["fwd_twist"]))
    zl = limbs_bf16(z, 2).reshape(entries * FIRST, 3 * SECOND)
    y2 = lax.dot_general(
        jnp.asarray(tables["fwd2"].T, jnp.bfloat16),
        zl,
        (((1,), (1,)), ((), ())),
        preferred_element_type=jnp.float32,
    )
    return fold3(y2[0:SECOND], y2[SECOND : 2 * SECOND], y2[2 * SECOND :])


def inverse(pv, tables):
    entries = pv.shape[0]
    pl_ = limbs_bf16(pv, 2)
    y = jnp.einsum(
        "ecK,KN->ecN", pl_, jnp.asarray(tables["inv1"], jnp.bfloat16), preferred_element_type=jnp.float32
    )
    z = fold3(y[..., 0:SECOND], y[..., SECOND : 2 * SECOND], y[..., 2 * SECOND :])
    z = twist(z, jnp.asarray(tables["inv_twist"]))
    zl = limbs_bf16(z, 1)
    y2 = jnp.einsum(
        "eLb,NL->eNb", zl, jnp.asarray(tables["inv2"], jnp.bfloat16), preferred_element_type=jnp.float32
    )
    out = fold3(y2[:, 0:FIRST], y2[:, FIRST : 2 * FIRST], y2[:, 2 * FIRST :])
    return out.reshape(entries, LENGTH)


def balanced3(x):
    h = jnp.floor((x + 128.0) * (1.0 / 256.0))
    x0 = x - 256.0 * h
    h2 = jnp.floor((h + 128.0) * (1.0 / 256.0))
    x1 = h - 256.0 * h2
    return x0, x1, h2


def multiply_points(left, right):
    x0, x1, x2 = split3(left)
    zero = jnp.zeros_like(left)
    scaled = [left, fold3(zero, x0, x1 + 256.0 * x2), fold3(zero, zero, left)]
    limbs = [balanced3(v) for v in scaled]
    rows = [jnp.concatenate([limbs[y][u].astype(jnp.bfloat16) for y in range(3)], axis=2) for u in range(3)]
    stacked = jnp.concatenate(rows, axis=1)
    right_limbs = limbs_bf16(right, 2)
    levels = jnp.einsum("pak,pjk->paj", stacked, right_limbs, preferred_element_type=jnp.float32)
    n_i = left.shape[1]
    return fold3(levels[:, 0:n_i], levels[:, n_i : 2 * n_i], levels[:, 2 * n_i :])


def make_body(n_grp, n_pt, n_chunks):
    tables = build_tables()
    d_local = SECOND // n_pt

    def body(left_factor, right_factor):
        il, kl, _ = left_factor.shape
        jl = right_factor.shape[0]

        def to_points(x, rows):
            ev = forward(x.reshape(rows * kl, -1), tables)
            ev = ev.reshape(n_pt, d_local, rows * kl * FIRST)
            ev = lax.all_to_all(ev, "pt", split_axis=0, concat_axis=0, tiled=False)
            return ev.reshape(n_pt, d_local, rows, kl, FIRST)

        jc = jl // n_chunks
        left_pts = to_points(left_factor, il)
        right_recv = [to_points(right_factor[0:jc], jc)]
        left_pts, right_recv[0] = lax.optimization_barrier((left_pts, right_recv[0]))
        left_pts = jnp.broadcast_to(left_pts[None], (n_grp,) + left_pts.shape)
        left_pts = lax.all_to_all(left_pts, "grp", split_axis=0, concat_axis=0, tiled=True)
        left_pts = jnp.transpose(left_pts, (2, 5, 0, 3, 1, 4))
        left_pts = left_pts.reshape(d_local * FIRST, n_grp * il, n_pt * kl)
        prods = []
        for chunk in range(n_chunks):
            if chunk + 1 < n_chunks:
                ev = forward(right_factor[(chunk + 1) * jc : (chunk + 2) * jc].reshape(jc * kl, -1), tables)
                ev = ev.reshape(n_pt, d_local, jc * kl * FIRST)
                left_pts, ev = lax.optimization_barrier((left_pts, ev))
                ev = lax.all_to_all(ev, "pt", split_axis=0, concat_axis=0, tiled=False)
                right_recv.append(ev.reshape(n_pt, d_local, jc, kl, FIRST))
            right_pts = jnp.transpose(right_recv[chunk], (1, 4, 2, 0, 3)).reshape(d_local * FIRST, jc, n_pt * kl)
            prods.append(multiply_points(left_pts, right_pts))
        prod = jnp.concatenate(prods, axis=2) if n_chunks > 1 else prods[0]
        n_i = prod.shape[1]
        ib = n_i // n_grp
        jb = n_grp * jl // n_pt
        prod = prod.reshape(d_local * FIRST, n_grp, ib, jl)
        prod = lax.all_to_all(prod, "grp", split_axis=1, concat_axis=1, tiled=True)
        prod = jnp.transpose(prod, (0, 2, 1, 3)).reshape(d_local, FIRST, ib, n_pt, jb)
        prod = jnp.transpose(prod, (3, 0, 1, 2, 4))
        prod = lax.all_to_all(prod, "pt", split_axis=0, concat_axis=0, tiled=False)
        pv = jnp.transpose(prod, (3, 4, 2, 0, 1)).reshape(ib * jb, FIRST, SECOND)
        coeffs = inverse(pv, tables)
        return (coeffs / float(modulus)).reshape(ib, jb, LENGTH)

    return body


def solution(mesh):
    n_grp = mesh.shape["grp"]
    n_pt = mesh.shape["pt"]
    return jax.shard_map(
        make_body(n_grp, n_pt, 2),
        mesh=mesh,
        in_specs=(P("grp", "pt", None), P("grp", "pt", None)),
        out_specs=P("grp", "pt", None),
        check_vma=False,
    )
```

```python
import jax
import jax.numpy as jnp
import numpy as np
from jax import lax
from jax.sharding import PartitionSpec as P

FIRST = 32
SECOND = 128
HALF_FIRST = FIRST // 2
LENGTH = FIRST * SECOND

modulus = 7340033
INV_P = float(np.float32(1.0 / modulus))


def root_powers(length_all):
    for generator in range(2, 64):
        candidate = pow(generator, (modulus - 1) // length_all, modulus)
        if pow(candidate, length_all // 2, modulus) == modulus - 1:
            break
    powers = [1]
    for counter in range(length_all - 1):
        powers.append(powers[-1] * candidate % modulus)
    return np.array(powers, dtype=np.int64)


def balanced_limbs(values):
    v = np.asarray(values, dtype=np.int64)
    l0 = (v + 128) % 256 - 128
    v = (v - l0) // 256
    l1 = (v + 128) % 256 - 128
    l2 = (v - l1) // 256
    return [l0, l1, l2]


def scaled_stack(table):
    n, k = table.shape
    out = np.zeros((3, n, 3, k), dtype=np.float32)
    for level in range(3):
        scaled = table * pow(256, level, modulus) % modulus
        for limb, piece in enumerate(balanced_limbs(scaled)):
            out[limb, :, level, :] = piece
    return out.reshape(3 * n, 3 * k)


def twist_stack(table):
    out = np.zeros((3, 3) + table.shape, dtype=np.float32)
    for level in range(3):
        scaled = table * pow(256, level, modulus) % modulus
        for limb, piece in enumerate(balanced_limbs(scaled)):
            out[level, limb] = piece
    return out


def build_tables():
    powers = root_powers(LENGTH)

    def pw(e):
        return powers[np.asarray(e) % LENGTH]

    a16 = np.arange(HALF_FIRST)
    c32 = np.arange(FIRST)
    b128 = np.arange(SECOND)
    scale_inv = pow(LENGTH, modulus - 2, modulus)
    fwd1 = pw(SECOND * np.outer(c32, a16))
    fwd_twist = pw(np.outer(c32, b128))
    fwd2 = pw(FIRST * np.outer(b128, b128))
    inv1 = pw(-FIRST * np.outer(b128, b128))
    inv_twist = pw(-np.outer(c32, b128))
    inv2 = pw(-SECOND * np.outer(c32, c32)) * scale_inv % modulus
    return dict(
        fwd1=scaled_stack(fwd1),
        fwd_twist=twist_stack(fwd_twist),
        fwd2=scaled_stack(fwd2).T.copy(),
        inv1=scaled_stack(inv1).T.copy(),
        inv_twist=twist_stack(inv_twist),
        inv2=scaled_stack(inv2),
    )


def split3(x):
    h = jnp.floor(x * (1.0 / 256.0))
    x0 = x - 256.0 * h
    x2 = jnp.floor(h * (1.0 / 256.0))
    x1 = h - 256.0 * x2
    return x0, x1, x2


def fold3(s0, s1, s2):
    f = s2 * 65536.0 + s1 * 256.0 + s0
    q = jnp.round(f * INV_P)
    d = s2 - 112.0 * q
    e = s1 + 256.0 * d
    r = s0 + 256.0 * e - q
    return jnp.where(r < 0, r + float(modulus), r)


def twist(z, tw):
    zl = split3(z)
    s = [zl[0] * tw[0, u] + zl[1] * tw[1, u] + zl[2] * tw[2, u] for u in range(3)]
    return fold3(*s)


def limbs_bf16(x, axis):
    return jnp.concatenate([piece.astype(jnp.bfloat16) for piece in split3(x)], axis=axis)


def forward(x, tables):
    entries = x.shape[0]
    x = x.reshape(entries, HALF_FIRST, SECOND)
    xl = limbs_bf16(x, 1)
    y = jnp.einsum(
        "eLb,NL->eNb", xl, jnp.asarray(tables["fwd1"], jnp.bfloat16), preferred_element_type=jnp.float32
    )
    z = fold3(y[:, 0:FIRST], y[:, FIRST : 2 * FIRST], y[:, 2 * FIRST :])
    z = twist(z, jnp.asarray(tables["fwd_twist"]))
    zl = limbs_bf16(z, 2).reshape(entries * FIRST, 3 * SECOND)
    y2 = lax.dot_general(
        jnp.asarray(tables["fwd2"].T, jnp.bfloat16),
        zl,
        (((1,), (1,)), ((), ())),
        preferred_element_type=jnp.float32,
    )
    return fold3(y2[0:SECOND], y2[SECOND : 2 * SECOND], y2[2 * SECOND :])


def inverse(pv, tables):
    entries = pv.shape[0]
    pl_ = limbs_bf16(pv, 2)
    y = jnp.einsum(
        "ecK,KN->ecN", pl_, jnp.asarray(tables["inv1"], jnp.bfloat16), preferred_element_type=jnp.float32
    )
    z = fold3(y[..., 0:SECOND], y[..., SECOND : 2 * SECOND], y[..., 2 * SECOND :])
    z = twist(z, jnp.asarray(tables["inv_twist"]))
    zl = limbs_bf16(z, 1)
    y2 = jnp.einsum(
        "eLb,NL->eNb", zl, jnp.asarray(tables["inv2"], jnp.bfloat16), preferred_element_type=jnp.float32
    )
    out = fold3(y2[:, 0:FIRST], y2[:, FIRST : 2 * FIRST], y2[:, 2 * FIRST :])
    return out.reshape(entries, LENGTH)


def balanced3(x):
    h = jnp.floor((x + 128.0) * (1.0 / 256.0))
    x0 = x - 256.0 * h
    h2 = jnp.floor((h + 128.0) * (1.0 / 256.0))
    x1 = h - 256.0 * h2
    return x0, x1, h2


def multiply_points(left, right):
    x0, x1, x2 = split3(left)
    zero = jnp.zeros_like(left)
    scaled = [left, fold3(zero, x0, x1 + 256.0 * x2), fold3(zero, zero, left)]
    limbs = [balanced3(v) for v in scaled]
    rows = [jnp.concatenate([limbs[y][u].astype(jnp.bfloat16) for y in range(3)], axis=2) for u in range(3)]
    stacked = jnp.concatenate(rows, axis=1)
    right_limbs = limbs_bf16(right, 2)
    levels = jnp.einsum("pak,pjk->paj", stacked, right_limbs, preferred_element_type=jnp.float32)
    n_i = left.shape[1]
    return fold3(levels[:, 0:n_i], levels[:, n_i : 2 * n_i], levels[:, 2 * n_i :])


def make_body(n_grp, n_pt, n_chunks):
    tables = build_tables()
    d_local = SECOND // n_pt

    def body(left_factor, right_factor):
        il, kl, _ = left_factor.shape
        jl = right_factor.shape[0]

        def to_points(x, rows):
            ev = forward(x.reshape(rows * kl, -1), tables)
            ev = ev.reshape(n_pt, d_local, rows * kl * FIRST)
            ev = lax.all_to_all(ev, "pt", split_axis=0, concat_axis=0, tiled=False)
            return ev.reshape(n_pt, d_local, rows, kl, FIRST)

        left_pts = to_points(left_factor, il)
        left_shape = left_pts.shape
        left_pts = jnp.broadcast_to(left_pts.reshape(1, -1, 128), (n_grp, left_pts.size // 128, 128))
        left_pts = lax.all_to_all(left_pts, "grp", split_axis=0, concat_axis=0, tiled=False)
        left_pts = left_pts.reshape((n_grp,) + left_shape)
        left_pts = jnp.transpose(left_pts, (2, 5, 0, 3, 1, 4))
        left_pts = left_pts.reshape(d_local * FIRST, n_grp * il, n_pt * kl)
        jc = jl // n_chunks
        prods = []
        for chunk in range(n_chunks):
            right_pts = to_points(right_factor[chunk * jc : (chunk + 1) * jc], jc)
            right_pts = jnp.transpose(right_pts, (1, 4, 2, 0, 3)).reshape(d_local * FIRST, jc, n_pt * kl)
            prods.append(multiply_points(left_pts, right_pts))
        prod = jnp.concatenate(prods, axis=2) if n_chunks > 1 else prods[0]
        n_i = prod.shape[1]
        ib = n_i // n_grp
        jb = n_grp * jl // n_pt
        n_pts = d_local * FIRST
        prod = jnp.transpose(prod.reshape(n_pts, n_grp, ib, jl), (1, 0, 2, 3))
        prod = prod.reshape(n_grp, n_pts * ib * jl // 128, 128)
        prod = lax.all_to_all(prod, "grp", split_axis=0, concat_axis=0, tiled=False)
        prod = prod.reshape(n_grp, d_local, FIRST, ib, jl)
        prod = jnp.transpose(prod, (1, 2, 3, 0, 4)).reshape(d_local, FIRST, ib, n_pt, jb)
        prod = jnp.transpose(prod, (3, 0, 1, 2, 4))
        prod = prod.reshape(n_pt, n_pts * ib * jb // 128, 128)
        prod = lax.all_to_all(prod, "pt", split_axis=0, concat_axis=0, tiled=False)
        prod = prod.reshape(n_pt, d_local, FIRST, ib, jb)
        pv = jnp.transpose(prod, (3, 4, 2, 0, 1)).reshape(ib * jb, FIRST, SECOND)
        coeffs = inverse(pv, tables)
        return (coeffs / float(modulus)).reshape(ib, jb, LENGTH)

    return body


def solution(mesh):
    n_grp = mesh.shape["grp"]
    n_pt = mesh.shape["pt"]
    return jax.shard_map(
        make_body(n_grp, n_pt, 2),
        mesh=mesh,
        in_specs=(P("grp", "pt", None), P("grp", "pt", None)),
        out_specs=P("grp", "pt", None),
        check_vma=False,
    )
```

```python
import jax
import jax.numpy as jnp
import numpy as np
from jax import lax
from jax.sharding import PartitionSpec as P

FIRST = 32
SECOND = 128
HALF_FIRST = FIRST // 2
LENGTH = FIRST * SECOND

modulus = 7340033
INV_P = float(np.float32(1.0 / modulus))


def root_powers(length_all):
    for generator in range(2, 64):
        candidate = pow(generator, (modulus - 1) // length_all, modulus)
        if pow(candidate, length_all // 2, modulus) == modulus - 1:
            break
    powers = [1]
    for counter in range(length_all - 1):
        powers.append(powers[-1] * candidate % modulus)
    return np.array(powers, dtype=np.int64)


def balanced_limbs(values):
    v = np.asarray(values, dtype=np.int64)
    l0 = (v + 128) % 256 - 128
    v = (v - l0) // 256
    l1 = (v + 128) % 256 - 128
    l2 = (v - l1) // 256
    return [l0, l1, l2]


def scaled_stack(table):
    n, k = table.shape
    out = np.zeros((3, n, 3, k), dtype=np.float32)
    for level in range(3):
        scaled = table * pow(256, level, modulus) % modulus
        for limb, piece in enumerate(balanced_limbs(scaled)):
            out[limb, :, level, :] = piece
    return out.reshape(3 * n, 3 * k)


def twist_stack(table):
    out = np.zeros((3, 3) + table.shape, dtype=np.float32)
    for level in range(3):
        scaled = table * pow(256, level, modulus) % modulus
        for limb, piece in enumerate(balanced_limbs(scaled)):
            out[level, limb] = piece
    return out


def build_tables():
    powers = root_powers(LENGTH)

    def pw(e):
        return powers[np.asarray(e) % LENGTH]

    a16 = np.arange(HALF_FIRST)
    c32 = np.arange(FIRST)
    b128 = np.arange(SECOND)
    scale_inv = pow(LENGTH, modulus - 2, modulus)
    fwd1 = pw(SECOND * np.outer(c32, a16))
    fwd_twist = pw(np.outer(c32, b128))
    fwd2 = pw(FIRST * np.outer(b128, b128))
    inv1 = pw(-FIRST * np.outer(b128, b128))
    inv_twist = pw(-np.outer(c32, b128))
    inv2 = pw(-SECOND * np.outer(c32, c32)) * scale_inv % modulus
    return dict(
        fwd1=scaled_stack(fwd1),
        fwd_twist=twist_stack(fwd_twist),
        fwd2=scaled_stack(fwd2).T.copy(),
        inv1=scaled_stack(inv1).T.copy(),
        inv_twist=twist_stack(inv_twist),
        inv2=scaled_stack(inv2),
    )


def split3(x):
    h = jnp.floor(x * (1.0 / 256.0))
    x0 = x - 256.0 * h
    x2 = jnp.floor(h * (1.0 / 256.0))
    x1 = h - 256.0 * x2
    return x0, x1, x2


def fold3(s0, s1, s2):
    f = s2 * 65536.0 + s1 * 256.0 + s0
    q = jnp.round(f * INV_P)
    d = s2 - 112.0 * q
    e = s1 + 256.0 * d
    r = s0 + 256.0 * e - q
    return jnp.where(r < 0, r + float(modulus), r)


def twist(z, tw):
    zl = split3(z)
    s = [zl[0] * tw[0, u] + zl[1] * tw[1, u] + zl[2] * tw[2, u] for u in range(3)]
    return fold3(*s)


def limbs_bf16(x, axis):
    return jnp.concatenate([piece.astype(jnp.bfloat16) for piece in split3(x)], axis=axis)


def forward(x, tables):
    entries = x.shape[0]
    x = x.reshape(entries, HALF_FIRST, SECOND)
    xl = limbs_bf16(x, 1)
    y = jnp.einsum(
        "eLb,NL->eNb", xl, jnp.asarray(tables["fwd1"], jnp.bfloat16), preferred_element_type=jnp.float32
    )
    z = fold3(y[:, 0:FIRST], y[:, FIRST : 2 * FIRST], y[:, 2 * FIRST :])
    z = twist(z, jnp.asarray(tables["fwd_twist"]))
    zl = limbs_bf16(z, 2).reshape(entries * FIRST, 3 * SECOND)
    y2 = lax.dot_general(
        jnp.asarray(tables["fwd2"].T, jnp.bfloat16),
        zl,
        (((1,), (1,)), ((), ())),
        preferred_element_type=jnp.float32,
    )
    return fold3(y2[0:SECOND], y2[SECOND : 2 * SECOND], y2[2 * SECOND :])


def inverse(pv, tables):
    entries = pv.shape[0]
    pl_ = limbs_bf16(pv, 2)
    y = jnp.einsum(
        "ecK,KN->ecN", pl_, jnp.asarray(tables["inv1"], jnp.bfloat16), preferred_element_type=jnp.float32
    )
    z = fold3(y[..., 0:SECOND], y[..., SECOND : 2 * SECOND], y[..., 2 * SECOND :])
    z = twist(z, jnp.asarray(tables["inv_twist"]))
    zl = limbs_bf16(z, 1)
    y2 = jnp.einsum(
        "eLb,NL->eNb", zl, jnp.asarray(tables["inv2"], jnp.bfloat16), preferred_element_type=jnp.float32
    )
    out = fold3(y2[:, 0:FIRST], y2[:, FIRST : 2 * FIRST], y2[:, 2 * FIRST :])
    return out.reshape(entries, LENGTH)


def balanced3(x):
    h = jnp.floor((x + 128.0) * (1.0 / 256.0))
    x0 = x - 256.0 * h
    h2 = jnp.floor((h + 128.0) * (1.0 / 256.0))
    x1 = h - 256.0 * h2
    return x0, x1, h2


def multiply_points(left, right):
    x0, x1, x2 = split3(left)
    zero = jnp.zeros_like(left)
    scaled = [left, fold3(zero, x0, x1 + 256.0 * x2), fold3(zero, zero, left)]
    limbs = [balanced3(v) for v in scaled]
    rows = [jnp.concatenate([limbs[y][u].astype(jnp.bfloat16) for y in range(3)], axis=2) for u in range(3)]
    stacked = jnp.concatenate(rows, axis=1)
    right_limbs = limbs_bf16(right, 2)
    levels = jnp.einsum("pak,pjk->paj", stacked, right_limbs, preferred_element_type=jnp.float32)
    n_i = left.shape[1]
    return fold3(levels[:, 0:n_i], levels[:, n_i : 2 * n_i], levels[:, 2 * n_i :])


def make_body(n_grp, n_pt, n_chunks):
    tables = build_tables()
    d_local = SECOND // n_pt

    def body(left_factor, right_factor):
        il, kl, _ = left_factor.shape
        jl = right_factor.shape[0]

        def to_points(x, rows):
            ev = forward(x.reshape(rows * kl, -1), tables)
            ev = ev.reshape(n_pt, d_local, rows * kl * FIRST)
            ev = lax.all_to_all(ev, "pt", split_axis=0, concat_axis=0, tiled=False)
            return ev.reshape(n_pt, d_local, rows, kl, FIRST)

        left_pts = to_points(left_factor, il)
        left_shape = left_pts.shape
        left_pts = jnp.broadcast_to(left_pts.reshape(1, -1, 128), (n_grp, left_pts.size // 128, 128))
        left_pts = lax.all_to_all(left_pts, "grp", split_axis=0, concat_axis=0, tiled=False)
        left_pts = left_pts.reshape((n_grp,) + left_shape)
        left_pts = jnp.transpose(left_pts, (2, 5, 0, 3, 1, 4))
        left_pts = left_pts.reshape(d_local * FIRST, n_grp * il, n_pt * kl)
        jc = jl // n_chunks
        n_i = n_grp * il
        ib = n_i // n_grp
        jb = n_grp * jl // n_pt
        n_pts = d_local * FIRST
        prods = []
        for chunk in range(n_chunks):
            right_pts = to_points(right_factor[chunk * jc : (chunk + 1) * jc], jc)
            right_pts = jnp.transpose(right_pts, (1, 4, 2, 0, 3)).reshape(d_local * FIRST, jc, n_pt * kl)
            part = multiply_points(left_pts, right_pts)
            part = jnp.transpose(part.reshape(n_pts, n_grp, ib, jc), (1, 0, 2, 3))
            part = part.reshape(n_grp, n_pts * ib * jc // 128, 128)
            part = lax.all_to_all(part, "grp", split_axis=0, concat_axis=0, tiled=False)
            prods.append(part.reshape(n_grp, n_pts, ib, jc))
        prod = jnp.concatenate(prods, axis=3) if n_chunks > 1 else prods[0]
        prod = prod.reshape(n_grp, d_local, FIRST, ib, jl)
        prod = jnp.transpose(prod, (1, 2, 3, 0, 4)).reshape(d_local, FIRST, ib, n_pt, jb)
        prod = jnp.transpose(prod, (3, 0, 1, 2, 4))
        prod = prod.reshape(n_pt, n_pts * ib * jb // 128, 128)
        prod = lax.all_to_all(prod, "pt", split_axis=0, concat_axis=0, tiled=False)
        prod = prod.reshape(n_pt, d_local, FIRST, ib, jb)
        pv = jnp.transpose(prod, (3, 4, 2, 0, 1)).reshape(ib * jb, FIRST, SECOND)
        coeffs = inverse(pv, tables)
        return (coeffs / float(modulus)).reshape(ib, jb, LENGTH)

    return body


def solution(mesh):
    n_grp = mesh.shape["grp"]
    n_pt = mesh.shape["pt"]
    return jax.shard_map(
        make_body(n_grp, n_pt, 2),
        mesh=mesh,
        in_specs=(P("grp", "pt", None), P("grp", "pt", None)),
        out_specs=P("grp", "pt", None),
        check_vma=False,
    )
```

```python
import jax
import jax.numpy as jnp
import numpy as np
from jax import lax
from jax.sharding import PartitionSpec as P

FIRST = 32
SECOND = 128
HALF_FIRST = FIRST // 2
LENGTH = FIRST * SECOND

modulus = 7340033
INV_P = float(np.float32(1.0 / modulus))


def root_powers(length_all):
    for generator in range(2, 64):
        candidate = pow(generator, (modulus - 1) // length_all, modulus)
        if pow(candidate, length_all // 2, modulus) == modulus - 1:
            break
    powers = [1]
    for counter in range(length_all - 1):
        powers.append(powers[-1] * candidate % modulus)
    return np.array(powers, dtype=np.int64)


def balanced_limbs(values):
    v = np.asarray(values, dtype=np.int64)
    l0 = (v + 128) % 256 - 128
    v = (v - l0) // 256
    l1 = (v + 128) % 256 - 128
    l2 = (v - l1) // 256
    return [l0, l1, l2]


def scaled_stack(table):
    n, k = table.shape
    out = np.zeros((3, n, 3, k), dtype=np.float32)
    for level in range(3):
        scaled = table * pow(256, level, modulus) % modulus
        for limb, piece in enumerate(balanced_limbs(scaled)):
            out[limb, :, level, :] = piece
    return out.reshape(3 * n, 3 * k)


def twist_stack(table):
    out = np.zeros((3, 3) + table.shape, dtype=np.float32)
    for level in range(3):
        scaled = table * pow(256, level, modulus) % modulus
        for limb, piece in enumerate(balanced_limbs(scaled)):
            out[level, limb] = piece
    return out


def build_tables():
    powers = root_powers(LENGTH)

    def pw(e):
        return powers[np.asarray(e) % LENGTH]

    a16 = np.arange(HALF_FIRST)
    c32 = np.arange(FIRST)
    b128 = np.arange(SECOND)
    scale_inv = pow(LENGTH, modulus - 2, modulus)
    fwd1 = pw(SECOND * np.outer(c32, a16))
    fwd_twist = pw(np.outer(c32, b128))
    fwd2 = pw(FIRST * np.outer(b128, b128))
    inv1 = pw(-FIRST * np.outer(b128, b128))
    inv_twist = pw(-np.outer(c32, b128))
    inv2 = pw(-SECOND * np.outer(c32, c32)) * scale_inv % modulus
    return dict(
        fwd1=scaled_stack(fwd1),
        fwd_twist=twist_stack(fwd_twist),
        fwd2=scaled_stack(fwd2).T.copy(),
        inv1=scaled_stack(inv1).T.copy(),
        inv_twist=twist_stack(inv_twist),
        inv2=scaled_stack(inv2),
    )


def split3(x):
    h = jnp.floor(x * (1.0 / 256.0))
    x0 = x - 256.0 * h
    x2 = jnp.floor(h * (1.0 / 256.0))
    x1 = h - 256.0 * x2
    return x0, x1, x2


def fold3(s0, s1, s2):
    f = s2 * 65536.0 + s1 * 256.0 + s0
    q = jnp.round(f * INV_P)
    d = s2 - 112.0 * q
    e = s1 + 256.0 * d
    r = s0 + 256.0 * e - q
    return jnp.where(r < 0, r + float(modulus), r)


def twist(z, tw):
    zl = split3(z)
    s = [zl[0] * tw[0, u] + zl[1] * tw[1, u] + zl[2] * tw[2, u] for u in range(3)]
    return fold3(*s)


def limbs_bf16(x, axis):
    return jnp.concatenate([piece.astype(jnp.bfloat16) for piece in split3(x)], axis=axis)


def forward(x, tables):
    entries = x.shape[0]
    x = x.reshape(entries, HALF_FIRST, SECOND)
    xl = limbs_bf16(x, 1)
    y = jnp.einsum(
        "eLb,NL->eNb", xl, jnp.asarray(tables["fwd1"], jnp.bfloat16), preferred_element_type=jnp.float32
    )
    z = fold3(y[:, 0:FIRST], y[:, FIRST : 2 * FIRST], y[:, 2 * FIRST :])
    z = twist(z, jnp.asarray(tables["fwd_twist"]))
    zl = limbs_bf16(z, 2).reshape(entries * FIRST, 3 * SECOND)
    y2 = lax.dot_general(
        jnp.asarray(tables["fwd2"].T, jnp.bfloat16),
        zl,
        (((1,), (1,)), ((), ())),
        preferred_element_type=jnp.float32,
    )
    return fold3(y2[0:SECOND], y2[SECOND : 2 * SECOND], y2[2 * SECOND :])


def inverse(pv, tables):
    entries = pv.shape[0]
    pl_ = limbs_bf16(pv, 2)
    y = jnp.einsum(
        "ecK,KN->ecN", pl_, jnp.asarray(tables["inv1"], jnp.bfloat16), preferred_element_type=jnp.float32
    )
    z = fold3(y[..., 0:SECOND], y[..., SECOND : 2 * SECOND], y[..., 2 * SECOND :])
    z = twist(z, jnp.asarray(tables["inv_twist"]))
    zl = limbs_bf16(z, 1)
    y2 = jnp.einsum(
        "eLb,NL->eNb", zl, jnp.asarray(tables["inv2"], jnp.bfloat16), preferred_element_type=jnp.float32
    )
    out = fold3(y2[:, 0:FIRST], y2[:, FIRST : 2 * FIRST], y2[:, 2 * FIRST :])
    return out.reshape(entries, LENGTH)


def balanced3(x):
    h = jnp.floor((x + 128.0) * (1.0 / 256.0))
    x0 = x - 256.0 * h
    h2 = jnp.floor((h + 128.0) * (1.0 / 256.0))
    x1 = h - 256.0 * h2
    return x0, x1, h2


def multiply_points(left, right):
    x0, x1, x2 = split3(left)
    zero = jnp.zeros_like(left)
    scaled = [left, fold3(zero, x0, x1 + 256.0 * x2), fold3(zero, zero, left)]
    limbs = [balanced3(v) for v in scaled]
    rows = [jnp.concatenate([limbs[y][u].astype(jnp.bfloat16) for y in range(3)], axis=2) for u in range(3)]
    stacked = jnp.concatenate(rows, axis=1)
    right_limbs = limbs_bf16(right, 2)
    levels = jnp.einsum("pak,pjk->paj", stacked, right_limbs, preferred_element_type=jnp.float32)
    n_i = left.shape[1]
    return fold3(levels[:, 0:n_i], levels[:, n_i : 2 * n_i], levels[:, 2 * n_i :])


def make_body(n_grp, n_pt, n_chunks):
    tables = build_tables()
    d_local = SECOND // n_pt

    def body(left_factor, right_factor):
        il, kl, _ = left_factor.shape
        jl = right_factor.shape[0]

        def to_points(x, rows):
            ev = forward(x.reshape(rows * kl, -1), tables)
            ev = ev.reshape(n_pt, d_local, rows * kl * FIRST)
            ev = lax.all_to_all(ev, "pt", split_axis=0, concat_axis=0, tiled=False)
            return ev.reshape(n_pt, d_local, rows, kl, FIRST)

        left_all = lax.all_gather(left_factor, "grp", axis=0, tiled=True)
        left_pts = to_points(left_all, n_grp * il)
        left_pts = jnp.transpose(left_pts, (1, 4, 2, 0, 3))
        left_pts = left_pts.reshape(d_local * FIRST, n_grp * il, n_pt * kl)
        jc = jl // n_chunks
        prods = []
        for chunk in range(n_chunks):
            right_pts = to_points(right_factor[chunk * jc : (chunk + 1) * jc], jc)
            right_pts = jnp.transpose(right_pts, (1, 4, 2, 0, 3)).reshape(d_local * FIRST, jc, n_pt * kl)
            prods.append(multiply_points(left_pts, right_pts))
        prod = jnp.concatenate(prods, axis=2) if n_chunks > 1 else prods[0]
        n_i = prod.shape[1]
        ib = n_i // n_grp
        jb = n_grp * jl // n_pt
        n_pts = d_local * FIRST
        prod = jnp.transpose(prod.reshape(n_pts, n_grp, ib, jl), (1, 0, 2, 3))
        prod = prod.reshape(n_grp, n_pts * ib * jl // 128, 128)
        prod = lax.all_to_all(prod, "grp", split_axis=0, concat_axis=0, tiled=False)
        prod = prod.reshape(n_grp, d_local, FIRST, ib, jl)
        prod = jnp.transpose(prod, (1, 2, 3, 0, 4)).reshape(d_local, FIRST, ib, n_pt, jb)
        prod = jnp.transpose(prod, (3, 0, 1, 2, 4))
        prod = prod.reshape(n_pt, n_pts * ib * jb // 128, 128)
        prod = lax.all_to_all(prod, "pt", split_axis=0, concat_axis=0, tiled=False)
        prod = prod.reshape(n_pt, d_local, FIRST, ib, jb)
        pv = jnp.transpose(prod, (3, 4, 2, 0, 1)).reshape(ib * jb, FIRST, SECOND)
        coeffs = inverse(pv, tables)
        return (coeffs / float(modulus)).reshape(ib, jb, LENGTH)

    return body


def solution(mesh):
    n_grp = mesh.shape["grp"]
    n_pt = mesh.shape["pt"]
    return jax.shard_map(
        make_body(n_grp, n_pt, 2),
        mesh=mesh,
        in_specs=(P("grp", "pt", None), P("grp", "pt", None)),
        out_specs=P("grp", "pt", None),
        check_vma=False,
    )
```

```python
import jax
import jax.numpy as jnp
import numpy as np
from jax import lax
from jax.sharding import PartitionSpec as P

FIRST = 32
SECOND = 128
HALF_FIRST = FIRST // 2
LENGTH = FIRST * SECOND

modulus = 7340033
INV_P = float(np.float32(1.0 / modulus))


def root_powers(length_all):
    for generator in range(2, 64):
        candidate = pow(generator, (modulus - 1) // length_all, modulus)
        if pow(candidate, length_all // 2, modulus) == modulus - 1:
            break
    powers = [1]
    for counter in range(length_all - 1):
        powers.append(powers[-1] * candidate % modulus)
    return np.array(powers, dtype=np.int64)


def balanced_limbs(values):
    v = np.asarray(values, dtype=np.int64)
    l0 = (v + 128) % 256 - 128
    v = (v - l0) // 256
    l1 = (v + 128) % 256 - 128
    l2 = (v - l1) // 256
    return [l0, l1, l2]


def scaled_stack(table):
    n, k = table.shape
    out = np.zeros((3, n, 3, k), dtype=np.float32)
    for level in range(3):
        scaled = table * pow(256, level, modulus) % modulus
        for limb, piece in enumerate(balanced_limbs(scaled)):
            out[limb, :, level, :] = piece
    return out.reshape(3 * n, 3 * k)


def twist_stack(table):
    out = np.zeros((3, 3) + table.shape, dtype=np.float32)
    for level in range(3):
        scaled = table * pow(256, level, modulus) % modulus
        for limb, piece in enumerate(balanced_limbs(scaled)):
            out[level, limb] = piece
    return out


def build_tables():
    powers = root_powers(LENGTH)

    def pw(e):
        return powers[np.asarray(e) % LENGTH]

    a16 = np.arange(HALF_FIRST)
    c32 = np.arange(FIRST)
    b128 = np.arange(SECOND)
    scale_inv = pow(LENGTH, modulus - 2, modulus)
    fwd1 = pw(SECOND * np.outer(c32, a16))
    fwd_twist = pw(np.outer(c32, b128))
    fwd2 = pw(FIRST * np.outer(b128, b128))
    inv1 = pw(-FIRST * np.outer(b128, b128))
    inv_twist = pw(-np.outer(c32, b128))
    inv2 = pw(-SECOND * np.outer(c32, c32)) * scale_inv % modulus
    return dict(
        fwd1=scaled_stack(fwd1),
        fwd_twist=twist_stack(fwd_twist),
        fwd2=scaled_stack(fwd2).T.copy(),
        inv1=scaled_stack(inv1).T.copy(),
        inv_twist=twist_stack(inv_twist),
        inv2=scaled_stack(inv2),
    )


def split3(x):
    h = jnp.floor(x * (1.0 / 256.0))
    x0 = x - 256.0 * h
    x2 = jnp.floor(h * (1.0 / 256.0))
    x1 = h - 256.0 * x2
    return x0, x1, x2


def fold3(s0, s1, s2):
    f = s2 * 65536.0 + s1 * 256.0 + s0
    q = jnp.round(f * INV_P)
    d = s2 - 112.0 * q
    e = s1 + 256.0 * d
    r = s0 + 256.0 * e - q
    return jnp.where(r < 0, r + float(modulus), r)


def twist(z, tw):
    zl = split3(z)
    s = [zl[0] * tw[0, u] + zl[1] * tw[1, u] + zl[2] * tw[2, u] for u in range(3)]
    return fold3(*s)


def limbs_bf16(x, axis):
    return jnp.concatenate([piece.astype(jnp.bfloat16) for piece in split3(x)], axis=axis)


def forward(x, tables):
    entries = x.shape[0]
    x = x.reshape(entries, HALF_FIRST, SECOND)
    xl = limbs_bf16(x, 1)
    y = jnp.einsum(
        "eLb,NL->eNb", xl, jnp.asarray(tables["fwd1"], jnp.bfloat16), preferred_element_type=jnp.float32
    )
    z = fold3(y[:, 0:FIRST], y[:, FIRST : 2 * FIRST], y[:, 2 * FIRST :])
    z = twist(z, jnp.asarray(tables["fwd_twist"]))
    zl = limbs_bf16(z, 2).reshape(entries * FIRST, 3 * SECOND)
    y2 = lax.dot_general(
        jnp.asarray(tables["fwd2"].T, jnp.bfloat16),
        zl,
        (((1,), (1,)), ((), ())),
        preferred_element_type=jnp.float32,
    )
    return fold3(y2[0:SECOND], y2[SECOND : 2 * SECOND], y2[2 * SECOND :])


def inverse(pv, tables):
    entries = pv.shape[0]
    pl_ = limbs_bf16(pv, 2)
    y = jnp.einsum(
        "ecK,KN->ecN", pl_, jnp.asarray(tables["inv1"], jnp.bfloat16), preferred_element_type=jnp.float32
    )
    z = fold3(y[..., 0:SECOND], y[..., SECOND : 2 * SECOND], y[..., 2 * SECOND :])
    z = twist(z, jnp.asarray(tables["inv_twist"]))
    zl = limbs_bf16(z, 1)
    y2 = jnp.einsum(
        "eLb,NL->eNb", zl, jnp.asarray(tables["inv2"], jnp.bfloat16), preferred_element_type=jnp.float32
    )
    out = fold3(y2[:, 0:FIRST], y2[:, FIRST : 2 * FIRST], y2[:, 2 * FIRST :])
    return out.reshape(entries, LENGTH)


def balanced3(x):
    h = jnp.floor((x + 128.0) * (1.0 / 256.0))
    x0 = x - 256.0 * h
    h2 = jnp.floor((h + 128.0) * (1.0 / 256.0))
    x1 = h - 256.0 * h2
    return x0, x1, h2


def multiply_points(left, right):
    x0, x1, x2 = split3(left)
    zero = jnp.zeros_like(left)
    scaled = [left, fold3(zero, x0, x1 + 256.0 * x2), fold3(zero, zero, left)]
    limbs = [balanced3(v) for v in scaled]
    rows = [jnp.concatenate([limbs[y][u].astype(jnp.bfloat16) for y in range(3)], axis=2) for u in range(3)]
    stacked = jnp.concatenate(rows, axis=1)
    right_limbs = limbs_bf16(right, 2)
    levels = jnp.einsum("pak,pjk->paj", stacked, right_limbs, preferred_element_type=jnp.float32)
    n_i = left.shape[1]
    return fold3(levels[:, 0:n_i], levels[:, n_i : 2 * n_i], levels[:, 2 * n_i :])


def make_body(n_grp, n_pt, n_chunks):
    tables = build_tables()
    d_local = SECOND // n_pt

    def body(left_factor, right_factor):
        il, kl, _ = left_factor.shape
        jl = right_factor.shape[0]

        def to_points(x, rows):
            ev = forward(x.reshape(rows * kl, -1), tables)
            ev = ev.reshape(n_pt, d_local, rows * kl * FIRST)
            ev = lax.all_to_all(ev, "pt", split_axis=0, concat_axis=0, tiled=False)
            return ev.reshape(n_pt, d_local, rows, kl, FIRST)

        jc = jl // n_chunks
        both = to_points(jnp.concatenate([left_factor, right_factor[0:jc]], axis=0), il + jc)
        left_pts = both[:, :, :il]
        first_right = both[:, :, il:]
        left_shape = left_pts.shape
        left_pts = jnp.broadcast_to(left_pts.reshape(1, -1, 128), (n_grp, left_pts.size // 128, 128))
        left_pts = lax.all_to_all(left_pts, "grp", split_axis=0, concat_axis=0, tiled=False)
        left_pts = left_pts.reshape((n_grp,) + left_shape)
        left_pts = jnp.transpose(left_pts, (2, 5, 0, 3, 1, 4))
        left_pts = left_pts.reshape(d_local * FIRST, n_grp * il, n_pt * kl)
        prods = []
        for chunk in range(n_chunks):
            if chunk == 0:
                right_pts = first_right
            else:
                right_pts = to_points(right_factor[chunk * jc : (chunk + 1) * jc], jc)
            right_pts = jnp.transpose(right_pts, (1, 4, 2, 0, 3)).reshape(d_local * FIRST, jc, n_pt * kl)
            prods.append(multiply_points(left_pts, right_pts))
        prod = jnp.concatenate(prods, axis=2) if n_chunks > 1 else prods[0]
        n_i = prod.shape[1]
        ib = n_i // n_grp
        jb = n_grp * jl // n_pt
        n_pts = d_local * FIRST
        prod = jnp.transpose(prod.reshape(n_pts, n_grp, ib, jl), (1, 0, 2, 3))
        prod = prod.reshape(n_grp, n_pts * ib * jl // 128, 128)
        prod = lax.all_to_all(prod, "grp", split_axis=0, concat_axis=0, tiled=False)
        prod = prod.reshape(n_grp, d_local, FIRST, ib, jl)
        prod = jnp.transpose(prod, (1, 2, 3, 0, 4)).reshape(d_local, FIRST, ib, n_pt, jb)
        prod = jnp.transpose(prod, (3, 0, 1, 2, 4))
        prod = prod.reshape(n_pt, n_pts * ib * jb // 128, 128)
        prod = lax.all_to_all(prod, "pt", split_axis=0, concat_axis=0, tiled=False)
        prod = prod.reshape(n_pt, d_local, FIRST, ib, jb)
        pv = jnp.transpose(prod, (3, 4, 2, 0, 1)).reshape(ib * jb, FIRST, SECOND)
        coeffs = inverse(pv, tables)
        return (coeffs / float(modulus)).reshape(ib, jb, LENGTH)

    return body


def solution(mesh):
    n_grp = mesh.shape["grp"]
    n_pt = mesh.shape["pt"]
    return jax.shard_map(
        make_body(n_grp, n_pt, 2),
        mesh=mesh,
        in_specs=(P("grp", "pt", None), P("grp", "pt", None)),
        out_specs=P("grp", "pt", None),
        check_vma=False,
    )
```
